128 devices in a mesh: dp: 4 (over z_hi, core), seq: 32 (over x, z_lo, y).
Axes of the slice: x: 4, y: 4, z: 4 (z_hi: 2, z_lo: 2; z = z_hi * 2 + z_lo), core: 2. Of those that a mesh axis runs over, the one named last changes fastest.
Arguments:
- frames_in: bfloat16 [4, 8192, 512], P('dp', 'seq'), may hold values from -6 to 6
- proj_weight: bfloat16 [512, 1536], replicated, may hold values from -0.25 to 0.25
- conv_taps: float32 [3, 1536], replicated, may hold values from -2.5 to 2.5
- long_filters: bfloat16 [8192, 2, 512], P('seq'), as said below
- out_grad: bfloat16 [4, 8192, 512], P('dp', 'seq'), may hold values from -6 to 6
Outputs:
- layer_out: bfloat16 [4, 8192, 512], P('dp', 'seq')
- grad_in: bfloat16 [4, 8192, 512], P('dp', 'seq')
- grad_proj: float32 [512, 1536], P(('dp', 'seq'))
- grad_taps: float32 [3, 1536], replicated
- grad_filters: float32 [8192, 2, 512], P('seq', None, 'dp')
The draws below stay inside these ranges and needn't reach their ends.
Inputs may be any that keep to these rules, and one draw needn't show every extreme that they name: `long_filters`: taps of the two long filters for every channel.
All inputs are finite; a program needn't handle non-finite values.
Results may differ from the reference program's by a relative error of at most 0.013.
Values may be sent and summed in bfloat16 or wider, within the bound.
No kernel may reach another device: no remote copies, remote signals or barrier semaphores. Data moves between devices by JAX's collectives and lax.ppermute only.
A program may use at most 192 MiB of HBM per device.

```python
import math
import jax
import jax.numpy as jnp
from jax import lax

D = 512
KS = 3
S = 256
RECS = 4
L = 8192
N_SEQ = 32


def draw_long_filters(key, part):
    rate_key = jax.random.fold_in(key, 11)
    noise_key = jax.random.fold_in(key, 23)
    rates = jnp.exp(jax.random.uniform(rate_key, (1, 2, D), jnp.float32, math.log(0.5), math.log(8.0)))
    positions = jnp.arange(L, dtype=jnp.float32)[:, None, None] / L
    envelope = jnp.exp(-rates * positions) * jnp.sqrt(2.0 * rates / L)
    noise = jnp.clip(jax.random.normal(noise_key, (L, 2, D), jnp.float32), -4.0, 4.0)
    return (noise * envelope).astype(jnp.bfloat16)


def with_spikes(result, own_key, source, target, blocks, factor):
    def block_of(axis_at):
        return (jnp.arange(result.shape[axis_at]) // (result.shape[axis_at] // blocks)).reshape((-1,) + (1,) * (result.ndim - 1 - axis_at))

    one_side = jax.random.permutation(own_key, blocks)[block_of(target)]
    second = (block_of(target) + blocks // 2) % blocks
    return jnp.where((block_of(source) == one_side) | (block_of(source) == second), factor * result, result)


def level_of(rng, shape, split, smallest, largest):
    def one(axis_at, parts):
        heights = jax.random.uniform(jax.random.fold_in(jax.random.fold_in(rng, 6), axis_at), (parts,), jnp.float32, smallest / len(split), largest / len(split))
        return jnp.repeat(jnp.exp(heights), shape[axis_at] // parts).reshape((-1,) + (1,) * (len(shape) - axis_at - 1))

    loudness = one(*split[0])
    for cut in split[1:]:
        loudness = loudness * one(*cut)
    return loudness


def bell_draw(stream_key, shape, spread, most, cuts=(), kind=jnp.bfloat16):
    factor_of = level_of(stream_key, shape, cuts, -0.22, 0.18) if cuts else 1.0
    array = jax.random.normal(stream_key, shape, jnp.float32) * spread * factor_of
    return jnp.minimum(jnp.maximum(array, -most), most).astype(kind)


def gaussian_with(key, extent, deviation, bound, pieces, heavy, kind=jnp.bfloat16):
    drawn = deviation * jax.random.normal(key, extent, jnp.float32)
    if pieces:
        drawn = drawn * level_of(key, extent, pieces, -0.22, 0.18)
    return jnp.clip(with_spikes(drawn, jax.random.fold_in(key, 3), *heavy), -bound, bound).astype(kind)


def setup_inputs(seed: int = 0) -> dict:
    splits = jax.random.split(jax.random.key(seed), 6)
    return {
        "frames_in": gaussian_with(splits[0], (RECS, L, D), 1.0, 6.0, ((0, 4), (1, 32)), (1, 2, 32, 2.75)),
        "proj_weight": bell_draw(splits[1], (D, 3 * D), D ** -0.5, 0.25),
        "conv_taps": bell_draw(splits[2], (KS, 3 * D), 0.6, 2.5, (), jnp.float32),
        "long_filters": draw_long_filters(jax.random.fold_in(splits[5], 71), 0),
        "out_grad": bell_draw(splits[4], (RECS, L, D), 1.0, 6.0, ((0, 4), (1, 32))),
    }


FULL_TURN = 2.0 * math.pi

def twiddles(direction):
    freq_rows = 2 * N_SEQ
    products = jnp.arange(freq_rows, dtype=jnp.int32)[:, None] * jnp.arange(S, dtype=jnp.int32)[None, :] % (freq_rows * S)
    angles = products.astype(jnp.float32) * (FULL_TURN / (freq_rows * S))
    return jnp.cos(angles)[:, :, None] + direction * 1j * jnp.sin(angles)[:, :, None]

def round_parts(values):
    real_part = lax.optimization_barrier(jnp.real(values).astype(jnp.bfloat16)).astype(jnp.float32)
    imag_part = lax.optimization_barrier(jnp.imag(values).astype(jnp.bfloat16)).astype(jnp.float32)
    return real_part + 1j * imag_part

def spectrum(field):
    channels = field.shape[1]
    padded = jnp.concatenate([field.astype(jnp.float32), jnp.zeros((L, channels), jnp.float32)], axis=0)
    grid_view = padded.reshape(2 * N_SEQ, S, channels)
    section = round_parts(jnp.fft.fft(grid_view, axis=0) * twiddles(-1.0))
    return jnp.fft.fft(section, axis=1)

def restore(spectra, rounded):
    channels = spectra.shape[2]
    back = jnp.fft.ifft(spectra, axis=1) * twiddles(1.0)
    if rounded:
        back = round_parts(back)
    values = jnp.real(jnp.fft.ifft(back, axis=0))[:N_SEQ]
    return values.reshape(L, channels).astype(jnp.float32)

def reference(frames_in, proj_weight, conv_taps, long_filters, out_grad):
    grad_scale = 1.0 / math.sqrt(RECS * L)
    margin_rows = KS - 1
    filter_spectra = spectrum(long_filters.reshape(L, 2 * D))
    filter_one = filter_spectra[:, :, :D]
    filter_two = filter_spectra[:, :, D:]

    def one_recording(carry, inputs):
        signal, upstream = inputs
        projected = jnp.dot(signal, proj_weight, preferred_element_type=jnp.float32).astype(jnp.bfloat16)
        padded = jnp.concatenate([jnp.zeros((margin_rows, 3 * D), jnp.float32), projected.astype(jnp.float32)], axis=0)
        mixed = sum((conv_taps[tap_index][None, :] * padded[margin_rows - tap_index:margin_rows - tap_index + L] for tap_index in range(KS))).astype(jnp.bfloat16)
        value = mixed[:, :D]
        gate_one = mixed[:, D:2 * D].astype(jnp.float32)
        gate_two = mixed[:, 2 * D:].astype(jnp.float32)
        value_spectra = spectrum(value)
        conv_one = restore(filter_one * value_spectra, True).astype(jnp.bfloat16)
        first = (gate_one * conv_one.astype(jnp.float32)).astype(jnp.bfloat16)
        first_spectra = spectrum(first)
        conv_two = restore(filter_two * first_spectra, True).astype(jnp.bfloat16)
        layer_out = (gate_two * conv_two.astype(jnp.float32)).astype(jnp.bfloat16)
        upstream_f = upstream.astype(jnp.float32)
        grad_two = (upstream_f * gate_two).astype(jnp.bfloat16)
        two_spectra = spectrum(grad_two)
        grad_first = restore(jnp.conj(filter_two) * two_spectra, True).astype(jnp.bfloat16)
        grad_one = (grad_first.astype(jnp.float32) * gate_one).astype(jnp.bfloat16)
        one_spectra = spectrum(grad_one)
        grad_value = restore(jnp.conj(filter_one) * one_spectra, True).astype(jnp.bfloat16)
        grad_mixed = jnp.concatenate([grad_value.astype(jnp.float32), grad_first.astype(jnp.float32) * conv_one.astype(jnp.float32), upstream_f * conv_two.astype(jnp.float32)], axis=1).astype(jnp.bfloat16)
        grad_mixed_f = grad_mixed.astype(jnp.float32)
        grad_pad = jnp.concatenate([grad_mixed_f, jnp.zeros((margin_rows, 3 * D), jnp.float32)], axis=0)
        grad_rows = sum((conv_taps[tap_index][None, :] * grad_pad[tap_index:tap_index + L] for tap_index in range(KS))).astype(jnp.bfloat16)
        taps_terms = jnp.stack([lax.optimization_barrier(jnp.sum(padded[margin_rows - tap_index:margin_rows - tap_index + L] * grad_mixed_f, axis=0)) for tap_index in range(KS)])
        proj_terms = jnp.dot(signal.T, grad_rows, preferred_element_type=jnp.float32)
        grad_in = jnp.dot(grad_rows, proj_weight.T, preferred_element_type=jnp.float32).astype(jnp.bfloat16)
        pair_spectra = jnp.concatenate([jnp.conj(value_spectra) * one_spectra, jnp.conj(first_spectra) * two_spectra], axis=2)
        sum_real, sum_imag, proj_sum, taps_sum = carry
        carry = (sum_real + jnp.real(pair_spectra).astype(jnp.float32), sum_imag + jnp.imag(pair_spectra).astype(jnp.float32), proj_sum + proj_terms, taps_sum + taps_terms)
        return (carry, (layer_out, grad_in))
    start_carry = (jnp.zeros((2 * N_SEQ, S, 2 * D), jnp.float32), jnp.zeros((2 * N_SEQ, S, 2 * D), jnp.float32), jnp.zeros((D, 3 * D), jnp.float32), jnp.zeros((KS, 3 * D), jnp.float32))
    final_carry, stacked = lax.scan(one_recording, start_carry, (frames_in, out_grad))
    sum_real, sum_imag, proj_sum, taps_sum = final_carry
    grad_filters = (restore(sum_real + 1j * sum_imag, False) * grad_scale).reshape(L, 2, D).astype(jnp.float32)
    return (stacked[0], stacked[1], proj_sum * grad_scale, taps_sum * grad_scale, grad_filters)
```

```python
import math

import jax
import jax.numpy as jnp
from jax import lax
from jax.sharding import PartitionSpec as P

PRECISE = lax.Precision.HIGH
FULL_TURN = 2.0 * math.pi


def passed_along(value, axis, by):
    size = lax.axis_size(axis)
    pairs = [(i, i + by) for i in range(size) if 0 <= i + by < size]
    return lax.ppermute(value, axis, pairs)


def angle_table(row_count, col_count, period):
    products = (
        jnp.arange(row_count, dtype=jnp.int32)[:, None]
        * jnp.arange(col_count, dtype=jnp.int32)[None, :]
        % period
    )
    angles = products.astype(jnp.float32) * (FULL_TURN / period)
    return (jnp.cos(angles), jnp.sin(angles))


def rotate_stacked(stacked, cosine_table, sine_table, direction):
    return jnp.stack(
        [
            stacked[0] * cosine_table - direction * stacked[1] * sine_table,
            stacked[1] * cosine_table + direction * stacked[0] * sine_table,
        ]
    )


def dft_pair(cosine_table, sine_table, stacked, table_part, data_part, result_side, direction):
    block_table = jnp.stack(
        [
            jnp.stack([cosine_table, -direction * sine_table]),
            jnp.stack([direction * sine_table, cosine_table]),
        ]
    )
    return jnp.einsum(
        "yz" + table_part + ",z" + data_part + "->y" + result_side,
        block_table,
        stacked,
        precision=PRECISE,
    )


def spectral_product(left_side, right_side):
    return jnp.stack(
        [
            left_side[0] * right_side[0] - left_side[1] * right_side[1],
            left_side[0] * right_side[1] + left_side[1] * right_side[0],
        ]
    )


def adjoint_product(left_side, right_side):
    return jnp.stack(
        [
            left_side[0] * right_side[0] + left_side[1] * right_side[1],
            left_side[0] * right_side[1] - left_side[1] * right_side[0],
        ]
    )


def local_forward(stacked):
    local_freqs, frames, channels = (stacked.shape[1], stacked.shape[2], stacked.shape[3])
    inner_len = math.gcd(frames, 128)
    outer_len = frames // inner_len
    data = stacked.reshape(2, local_freqs, outer_len, inner_len, channels)
    cosine_table, sine_table = angle_table(outer_len, outer_len, outer_len)
    data = dft_pair(cosine_table, sine_table, data, "ga", "kabw", "kgbw", -1.0)
    cosine_table, sine_table = angle_table(outer_len, inner_len, frames)
    data = rotate_stacked(data, cosine_table[None, :, :, None], sine_table[None, :, :, None], -1.0)
    cosine_table, sine_table = angle_table(inner_len, inner_len, inner_len)
    data = dft_pair(cosine_table, sine_table, data, "fb", "kgbw", "kgfw", -1.0)
    return data.reshape(2, local_freqs, frames, channels)


def local_inverse(stacked):
    local_freqs, frames, channels = (stacked.shape[1], stacked.shape[2], stacked.shape[3])
    inner_len = math.gcd(frames, 128)
    outer_len = frames // inner_len
    data = stacked.reshape(2, local_freqs, outer_len, inner_len, channels)
    cosine_table, sine_table = angle_table(inner_len, inner_len, inner_len)
    data = dft_pair(cosine_table, sine_table, data, "bf", "kgfw", "kgbw", 1.0)
    cosine_table, sine_table = angle_table(outer_len, inner_len, frames)
    data = rotate_stacked(data, cosine_table[None, :, :, None], sine_table[None, :, :, None], 1.0)
    cosine_table, sine_table = angle_table(outer_len, outer_len, outer_len)
    data = dft_pair(cosine_table, sine_table, data, "ag", "kgbw", "kabw", 1.0)
    return data.reshape(2, local_freqs, frames, channels) / frames


def forward_transform(field):
    seq_devices = lax.axis_size("seq")
    frames, channels = field.shape
    block_rows = frames // seq_devices
    freq_rows = 2 * seq_devices
    fft_length = freq_rows * frames
    received = lax.all_to_all(
        field.reshape(seq_devices, block_rows, channels),
        "seq",
        split_axis=0,
        concat_axis=0,
        tiled=True,
    )
    values = received.astype(jnp.float32)
    cosine_table, sine_table = angle_table(freq_rows, seq_devices, freq_rows)
    part_table = jnp.stack([cosine_table, -sine_table])
    section = jnp.einsum("ykq,qrw->ykrw", part_table, values, precision=PRECISE)
    frame_ids = lax.axis_index("seq") * block_rows + jnp.arange(block_rows, dtype=jnp.int32)
    products = jnp.arange(freq_rows, dtype=jnp.int32)[:, None] * frame_ids[None, :] % fft_length
    angles = products.astype(jnp.float32) * (FULL_TURN / fft_length)
    stacked = rotate_stacked(
        section, jnp.cos(angles)[:, :, None], jnp.sin(angles)[:, :, None], -1.0
    ).astype(jnp.bfloat16)
    regrouped = lax.all_to_all(stacked, "seq", split_axis=1, concat_axis=2, tiled=True)
    return local_forward(regrouped.astype(jnp.float32))


def inverse_transform(spectra, keep_wide):
    seq_devices = lax.axis_size("seq")
    local_freqs, frames, channels = (spectra.shape[1], spectra.shape[2], spectra.shape[3])
    freq_rows = 2 * seq_devices
    fft_length = freq_rows * frames
    stacked = local_inverse(spectra)
    freq_ids = lax.axis_index("seq") * local_freqs + jnp.arange(local_freqs, dtype=jnp.int32)
    products = freq_ids[:, None] * jnp.arange(frames, dtype=jnp.int32)[None, :] % fft_length
    angles = products.astype(jnp.float32) * (FULL_TURN / fft_length)
    stacked = rotate_stacked(stacked, jnp.cos(angles)[:, :, None], jnp.sin(angles)[:, :, None], 1.0)
    if keep_wide:
        regrouped = lax.all_to_all(
            stacked.astype(jnp.bfloat16), "seq", split_axis=2, concat_axis=1, tiled=True
        ).astype(stacked.dtype)
    else:
        regrouped = lax.all_to_all(
            stacked.astype(jnp.bfloat16), "seq", split_axis=2, concat_axis=1, tiled=True
        ).astype(jnp.float32)
    cosine_table, sine_table = angle_table(seq_devices, freq_rows, freq_rows)
    part_table = jnp.stack([cosine_table, -sine_table])
    values = jnp.einsum("zqk,zkrw->qrw", part_table, regrouped, precision=PRECISE) / freq_rows
    if keep_wide:
        returned = lax.all_to_all(
            values.astype(jnp.bfloat16), "seq", split_axis=0, concat_axis=1, tiled=True
        ).astype(values.dtype)
    else:
        returned = lax.all_to_all(
            values.astype(jnp.bfloat16), "seq", split_axis=0, concat_axis=1, tiled=True
        )
    return returned.reshape(frames, channels)


def shards(frames_in, proj_weight, conv_taps, long_filters, out_grad):
    signal = frames_in[0]
    frames, channels = signal.shape
    seq_devices = lax.axis_size("seq")
    data_devices = lax.axis_size("dp")
    grad_scale = 1.0 / math.sqrt(data_devices * seq_devices * frames)
    margin_rows = conv_taps.shape[0] - 1
    tap_count = conv_taps.shape[0]
    projected = jnp.dot(signal, proj_weight, preferred_element_type=jnp.float32).astype(
        jnp.bfloat16
    )
    before = passed_along(projected[frames - margin_rows :], "seq", 1)
    extended = jnp.concatenate([before, projected], axis=0).astype(jnp.float32)
    mixed = sum(
        (
            conv_taps[tap_index][None, :]
            * extended[margin_rows - tap_index : margin_rows - tap_index + frames]
            for tap_index in range(tap_count)
        )
    ).astype(jnp.bfloat16)
    value = mixed[:, :channels]
    gate_one = mixed[:, channels : 2 * channels].astype(jnp.float32)
    gate_two = mixed[:, 2 * channels :].astype(jnp.float32)
    upstream = out_grad[0].astype(jnp.float32)
    grad_two = (upstream * gate_two).astype(jnp.bfloat16)
    opening = forward_transform(
        jnp.concatenate([long_filters.reshape(frames, 2 * channels), value, grad_two], axis=1)
    )
    filter_one = opening[..., :channels]
    filter_two = opening[..., channels : 2 * channels]
    value_spectra = opening[..., 2 * channels : 3 * channels]
    two_spectra = opening[..., 3 * channels :]
    middle_rows = inverse_transform(
        jnp.concatenate(
            [
                spectral_product(filter_one, value_spectra),
                adjoint_product(filter_two, two_spectra),
            ],
            axis=3,
        ),
        False,
    )
    conv_one = middle_rows[:, :channels]
    grad_first = middle_rows[:, channels:]
    first = (gate_one * conv_one.astype(jnp.float32)).astype(jnp.bfloat16)
    grad_one = (grad_first.astype(jnp.float32) * gate_one).astype(jnp.bfloat16)
    second = forward_transform(jnp.concatenate([first, grad_one], axis=1))
    first_spectra = second[..., :channels]
    one_spectra = second[..., channels:]
    closing = inverse_transform(
        jnp.concatenate(
            [
                spectral_product(filter_two, first_spectra),
                adjoint_product(filter_one, one_spectra),
                adjoint_product(value_spectra, one_spectra),
                adjoint_product(first_spectra, two_spectra),
            ],
            axis=3,
        ),
        False,
    )
    conv_two = closing[:, :channels]
    grad_value = closing[:, channels : 2 * channels]
    tap_rows = closing[:, 2 * channels :]
    block = channels // data_devices
    tap_blocks = tap_rows.reshape(frames, 2, data_devices, block).transpose(2, 1, 0, 3)
    tap_parts = lax.all_to_all(tap_blocks, "dp", split_axis=0, concat_axis=0, tiled=True)
    grad_filters = (
        jnp.sum(tap_parts.astype(jnp.float32), axis=0).transpose(1, 0, 2) * grad_scale
    )
    middle = (grad_first.astype(jnp.float32) * conv_one.astype(jnp.float32)).astype(jnp.bfloat16)
    layer_out = (gate_two * conv_two.astype(jnp.float32)).astype(jnp.bfloat16)
    grad_mixed = jnp.concatenate(
        [
            grad_value.astype(jnp.float32),
            middle.astype(jnp.float32),
            upstream * conv_two.astype(jnp.float32),
        ],
        axis=1,
    ).astype(jnp.bfloat16)
    after_rows = passed_along(grad_mixed[:margin_rows], "seq", -1)
    grad_mixed_f = grad_mixed.astype(jnp.float32)
    grad_pad = jnp.concatenate([grad_mixed, after_rows], axis=0).astype(jnp.float32)
    grad_rows = sum(
        (
            conv_taps[tap_index][None, :] * grad_pad[tap_index : tap_index + frames]
            for tap_index in range(tap_count)
        )
    ).astype(jnp.bfloat16)
    taps_terms = jnp.stack(
        [
            jnp.sum(
                extended[margin_rows - tap_index : margin_rows - tap_index + frames] * grad_mixed_f,
                axis=0,
            )
            for tap_index in range(tap_count)
        ]
    )
    grad_taps = lax.psum(taps_terms, ("dp", "seq")) * grad_scale
    proj_terms = jnp.einsum("tc,tj->cj", signal, grad_rows, preferred_element_type=jnp.float32)
    all_devices = data_devices * seq_devices
    proj_parts = lax.all_to_all(
        proj_terms.reshape(all_devices, proj_terms.shape[0] // all_devices, proj_terms.shape[1]),
        ("dp", "seq"),
        split_axis=0,
        concat_axis=0,
        tiled=True,
    )
    grad_proj = jnp.sum(proj_parts, axis=0) * grad_scale
    grad_in = jnp.einsum(
        "tj,dj->td", grad_rows, proj_weight, preferred_element_type=jnp.float32
    ).astype(jnp.bfloat16)
    return (layer_out[None], grad_in[None], grad_proj, grad_taps, grad_filters)


def solution(mesh):
    placed = (P("dp", "seq", None), P(), P(), P("seq", None, None), P("dp", "seq", None))
    return jax.shard_map(
        shards,
        mesh=mesh,
        in_specs=placed,
        out_specs=(
            P("dp", "seq", None),
            P("dp", "seq", None),
            P(("dp", "seq"), None),
            P(),
            P("seq", None, "dp"),
        ),
        check_vma=False,
    )
```

```python
import math

import jax
import jax.numpy as jnp
from jax import lax
from jax.sharding import PartitionSpec as P

PRECISE = lax.Precision.HIGH
FULL_TURN = 2.0 * math.pi


def passed_along(value, axis, by):
    size = lax.axis_size(axis)
    pairs = [(i, i + by) for i in range(size) if 0 <= i + by < size]
    return lax.ppermute(value, axis, pairs)


def angle_table(row_count, col_count, period):
    products = (
        jnp.arange(row_count, dtype=jnp.int32)[:, None]
        * jnp.arange(col_count, dtype=jnp.int32)[None, :]
        % period
    )
    angles = products.astype(jnp.float32) * (FULL_TURN / period)
    return (jnp.cos(angles), jnp.sin(angles))


def rotate_stacked(stacked, cosine_table, sine_table, direction):
    return jnp.stack(
        [
            stacked[0] * cosine_table - direction * stacked[1] * sine_table,
            stacked[1] * cosine_table + direction * stacked[0] * sine_table,
        ]
    )


def dft_pair(cosine_table, sine_table, stacked, table_part, data_part, result_side, direction):
    block_table = jnp.stack(
        [
            jnp.stack([cosine_table, -direction * sine_table]),
            jnp.stack([direction * sine_table, cosine_table]),
        ]
    )
    return jnp.einsum(
        "yz" + table_part + ",z" + data_part + "->y" + result_side,
        block_table,
        stacked,
        precision=PRECISE,
    )


def spectral_product(left_side, right_side):
    return jnp.stack(
        [
            left_side[0] * right_side[0] - left_side[1] * right_side[1],
            left_side[0] * right_side[1] + left_side[1] * right_side[0],
        ]
    )


def adjoint_product(left_side, right_side):
    return jnp.stack(
        [
            left_side[0] * right_side[0] + left_side[1] * right_side[1],
            left_side[0] * right_side[1] - left_side[1] * right_side[0],
        ]
    )


def local_forward(stacked):
    local_freqs, frames, channels = (stacked.shape[1], stacked.shape[2], stacked.shape[3])
    inner_len = math.gcd(frames, 128)
    outer_len = frames // inner_len
    data = stacked.reshape(2, local_freqs, outer_len, inner_len, channels)
    cosine_table, sine_table = angle_table(outer_len, outer_len, outer_len)
    data = dft_pair(cosine_table, sine_table, data, "ga", "kabw", "kgbw", -1.0)
    cosine_table, sine_table = angle_table(outer_len, inner_len, frames)
    data = rotate_stacked(data, cosine_table[None, :, :, None], sine_table[None, :, :, None], -1.0)
    cosine_table, sine_table = angle_table(inner_len, inner_len, inner_len)
    data = dft_pair(cosine_table, sine_table, data, "fb", "kgbw", "kgfw", -1.0)
    return data.reshape(2, local_freqs, frames, channels)


def local_inverse(stacked):
    local_freqs, frames, channels = (stacked.shape[1], stacked.shape[2], stacked.shape[3])
    inner_len = math.gcd(frames, 128)
    outer_len = frames // inner_len
    data = stacked.reshape(2, local_freqs, outer_len, inner_len, channels)
    cosine_table, sine_table = angle_table(inner_len, inner_len, inner_len)
    data = dft_pair(cosine_table, sine_table, data, "bf", "kgfw", "kgbw", 1.0)
    cosine_table, sine_table = angle_table(outer_len, inner_len, frames)
    data = rotate_stacked(data, cosine_table[None, :, :, None], sine_table[None, :, :, None], 1.0)
    cosine_table, sine_table = angle_table(outer_len, outer_len, outer_len)
    data = dft_pair(cosine_table, sine_table, data, "ag", "kgbw", "kabw", 1.0)
    return data.reshape(2, local_freqs, frames, channels) / frames


def forward_transform(field):
    seq_devices = lax.axis_size("seq")
    frames, channels = field.shape
    block_rows = frames // seq_devices
    freq_rows = 2 * seq_devices
    fft_length = freq_rows * frames
    received = lax.all_to_all(
        field.reshape(seq_devices, block_rows, channels),
        "seq",
        split_axis=0,
        concat_axis=0,
        tiled=True,
    )
    values = received.astype(jnp.float32)
    cosine_table, sine_table = angle_table(freq_rows, seq_devices, freq_rows)
    part_table = jnp.stack([cosine_table, -sine_table])
    section = jnp.einsum("ykq,qrw->ykrw", part_table, values, precision=PRECISE)
    frame_ids = lax.axis_index("seq") * block_rows + jnp.arange(block_rows, dtype=jnp.int32)
    products = jnp.arange(freq_rows, dtype=jnp.int32)[:, None] * frame_ids[None, :] % fft_length
    angles = products.astype(jnp.float32) * (FULL_TURN / fft_length)
    stacked = rotate_stacked(
        section, jnp.cos(angles)[:, :, None], jnp.sin(angles)[:, :, None], -1.0
    ).astype(jnp.bfloat16)
    regrouped = lax.all_to_all(stacked, "seq", split_axis=1, concat_axis=2, tiled=True)
    return local_forward(regrouped.astype(jnp.float32))


def inverse_transform(spectra, keep_wide):
    seq_devices = lax.axis_size("seq")
    local_freqs, frames, channels = (spectra.shape[1], spectra.shape[2], spectra.shape[3])
    freq_rows = 2 * seq_devices
    fft_length = freq_rows * frames
    stacked = local_inverse(spectra)
    freq_ids = lax.axis_index("seq") * local_freqs + jnp.arange(local_freqs, dtype=jnp.int32)
    products = freq_ids[:, None] * jnp.arange(frames, dtype=jnp.int32)[None, :] % fft_length
    angles = products.astype(jnp.float32) * (FULL_TURN / fft_length)
    stacked = rotate_stacked(stacked, jnp.cos(angles)[:, :, None], jnp.sin(angles)[:, :, None], 1.0)
    if keep_wide:
        regrouped = lax.all_to_all(
            stacked.astype(jnp.bfloat16), "seq", split_axis=2, concat_axis=1, tiled=True
        ).astype(stacked.dtype)
    else:
        regrouped = lax.all_to_all(
            stacked.astype(jnp.bfloat16), "seq", split_axis=2, concat_axis=1, tiled=True
        ).astype(jnp.float32)
    cosine_table, sine_table = angle_table(seq_devices, freq_rows, freq_rows)
    part_table = jnp.stack([cosine_table, -sine_table])
    values = jnp.einsum("zqk,zkrw->qrw", part_table, regrouped, precision=PRECISE) / freq_rows
    if keep_wide:
        returned = lax.all_to_all(
            values.astype(jnp.bfloat16), "seq", split_axis=0, concat_axis=1, tiled=True
        ).astype(values.dtype)
    else:
        returned = lax.all_to_all(
            values.astype(jnp.bfloat16), "seq", split_axis=0, concat_axis=1, tiled=True
        )
    return returned.reshape(frames, channels)


def shards(frames_in, proj_weight, conv_taps, long_filters, out_grad):
    signal = frames_in[0]
    frames, channels = signal.shape
    seq_devices = lax.axis_size("seq")
    data_devices = lax.axis_size("dp")
    grad_scale = 1.0 / math.sqrt(data_devices * seq_devices * frames)
    margin_rows = conv_taps.shape[0] - 1
    tap_count = conv_taps.shape[0]
    projected = jnp.dot(signal, proj_weight, preferred_element_type=jnp.float32).astype(
        jnp.bfloat16
    )
    before = passed_along(projected[frames - margin_rows :], "seq", 1)
    extended = jnp.concatenate([before, projected], axis=0).astype(jnp.float32)
    mixed = sum(
        (
            conv_taps[tap_index][None, :]
            * extended[margin_rows - tap_index : margin_rows - tap_index + frames]
            for tap_index in range(tap_count)
        )
    ).astype(jnp.bfloat16)
    value = mixed[:, :channels]
    gate_one = mixed[:, channels : 2 * channels].astype(jnp.float32)
    gate_two = mixed[:, 2 * channels :].astype(jnp.float32)
    upstream = out_grad[0].astype(jnp.float32)
    grad_two = (upstream * gate_two).astype(jnp.bfloat16)
    opening = forward_transform(
        jnp.concatenate([long_filters.reshape(frames, 2 * channels), value, grad_two], axis=1)
    )
    filter_one = opening[..., :channels]
    filter_two = opening[..., channels : 2 * channels]
    value_spectra = opening[..., 2 * channels : 3 * channels]
    two_spectra = opening[..., 3 * channels :]
    middle_rows = inverse_transform(
        jnp.concatenate(
            [
                spectral_product(filter_one, value_spectra),
                adjoint_product(filter_two, two_spectra),
            ],
            axis=3,
        ),
        False,
    )
    conv_one = middle_rows[:, :channels]
    grad_first = middle_rows[:, channels:]
    first = (gate_one * conv_one.astype(jnp.float32)).astype(jnp.bfloat16)
    grad_one = (grad_first.astype(jnp.float32) * gate_one).astype(jnp.bfloat16)
    second = forward_transform(jnp.concatenate([first, grad_one], axis=1))
    first_spectra = second[..., :channels]
    one_spectra = second[..., channels:]
    closing = inverse_transform(
        jnp.concatenate(
            [
                spectral_product(filter_two, first_spectra),
                adjoint_product(filter_one, one_spectra),
                adjoint_product(value_spectra, one_spectra),
                adjoint_product(first_spectra, two_spectra),
            ],
            axis=3,
        ),
        False,
    )
    conv_two = closing[:, :channels]
    grad_value = closing[:, channels : 2 * channels]
    tap_rows = closing[:, 2 * channels :]
    block = channels // data_devices
    tap_blocks = tap_rows.reshape(frames, 2, data_devices, block).transpose(2, 1, 0, 3)
    tap_parts = lax.all_to_all(tap_blocks, "dp", split_axis=0, concat_axis=0, tiled=True)
    grad_filters = (
        jnp.sum(tap_parts.astype(jnp.float32), axis=0).transpose(1, 0, 2) * grad_scale
    )
    middle = (grad_first.astype(jnp.float32) * conv_one.astype(jnp.float32)).astype(jnp.bfloat16)
    layer_out = (gate_two * conv_two.astype(jnp.float32)).astype(jnp.bfloat16)
    grad_mixed = jnp.concatenate(
        [
            grad_value.astype(jnp.float32),
            middle.astype(jnp.float32),
            upstream * conv_two.astype(jnp.float32),
        ],
        axis=1,
    ).astype(jnp.bfloat16)
    after_rows = passed_along(grad_mixed[:margin_rows], "seq", -1)
    grad_mixed_f = grad_mixed.astype(jnp.float32)
    grad_pad = jnp.concatenate([grad_mixed, after_rows], axis=0).astype(jnp.float32)
    grad_rows = sum(
        (
            conv_taps[tap_index][None, :] * grad_pad[tap_index : tap_index + frames]
            for tap_index in range(tap_count)
        )
    ).astype(jnp.bfloat16)
    taps_terms = jnp.stack(
        [
            jnp.sum(
                extended[margin_rows - tap_index : margin_rows - tap_index + frames] * grad_mixed_f,
                axis=0,
            )
            for tap_index in range(tap_count)
        ]
    )
    all_devices = data_devices * seq_devices
    taps_flat = taps_terms.reshape(all_devices, -1)
    taps_share = jnp.sum(
        lax.all_to_all(taps_flat, ("dp", "seq"), split_axis=0, concat_axis=0, tiled=True), axis=0
    )
    taps_whole = lax.all_to_all(
        jnp.broadcast_to(taps_share[None], taps_flat.shape),
        ("dp", "seq"),
        split_axis=0,
        concat_axis=0,
        tiled=True,
    )
    grad_taps = taps_whole.reshape(taps_terms.shape) * grad_scale
    proj_terms = jnp.einsum("tc,tj->cj", signal, grad_rows, preferred_element_type=jnp.float32)
    proj_parts = lax.all_to_all(
        proj_terms.reshape(all_devices, proj_terms.shape[0] // all_devices, proj_terms.shape[1]),
        ("dp", "seq"),
        split_axis=0,
        concat_axis=0,
        tiled=True,
    )
    grad_proj = jnp.sum(proj_parts, axis=0) * grad_scale
    grad_in = jnp.einsum(
        "tj,dj->td", grad_rows, proj_weight, preferred_element_type=jnp.float32
    ).astype(jnp.bfloat16)
    return (layer_out[None], grad_in[None], grad_proj, grad_taps, grad_filters)


def solution(mesh):
    placed = (P("dp", "seq", None), P(), P(), P("seq", None, None), P("dp", "seq", None))
    return jax.shard_map(
        shards,
        mesh=mesh,
        in_specs=placed,
        out_specs=(
            P("dp", "seq", None),
            P("dp", "seq", None),
            P(("dp", "seq"), None),
            P(),
            P("seq", None, "dp"),
        ),
        check_vma=False,
    )
```

```python
import math

import jax
import jax.numpy as jnp
from jax import lax
from jax.sharding import PartitionSpec as P

PRECISE = lax.Precision.HIGH
FULL_TURN = 2.0 * math.pi


def passed_along(value, axis, by):
    size = lax.axis_size(axis)
    pairs = [(i, i + by) for i in range(size) if 0 <= i + by < size]
    return lax.ppermute(value, axis, pairs)


def angle_table(row_count, col_count, period):
    products = (
        jnp.arange(row_count, dtype=jnp.int32)[:, None]
        * jnp.arange(col_count, dtype=jnp.int32)[None, :]
        % period
    )
    angles = products.astype(jnp.float32) * (FULL_TURN / period)
    return (jnp.cos(angles), jnp.sin(angles))


def rotate_stacked(stacked, cosine_table, sine_table, direction):
    return jnp.stack(
        [
            stacked[0] * cosine_table - direction * stacked[1] * sine_table,
            stacked[1] * cosine_table + direction * stacked[0] * sine_table,
        ]
    )


def dft_pair(cosine_table, sine_table, stacked, table_part, data_part, result_side, direction):
    block_table = jnp.stack(
        [
            jnp.stack([cosine_table, -direction * sine_table]),
            jnp.stack([direction * sine_table, cosine_table]),
        ]
    )
    return jnp.einsum(
        "yz" + table_part + ",z" + data_part + "->y" + result_side,
        block_table,
        stacked,
        precision=PRECISE,
    )


def spectral_product(left_side, right_side):
    return jnp.stack(
        [
            left_side[0] * right_side[0] - left_side[1] * right_side[1],
            left_side[0] * right_side[1] + left_side[1] * right_side[0],
        ]
    )


def adjoint_product(left_side, right_side):
    return jnp.stack(
        [
            left_side[0] * right_side[0] + left_side[1] * right_side[1],
            left_side[0] * right_side[1] - left_side[1] * right_side[0],
        ]
    )


def local_forward(stacked):
    local_freqs, frames, channels = (stacked.shape[1], stacked.shape[2], stacked.shape[3])
    inner_len = math.gcd(frames, 128)
    outer_len = frames // inner_len
    data = stacked.reshape(2, local_freqs, outer_len, inner_len, channels)
    cosine_table, sine_table = angle_table(outer_len, outer_len, outer_len)
    data = dft_pair(cosine_table, sine_table, data, "ga", "kabw", "kgbw", -1.0)
    cosine_table, sine_table = angle_table(outer_len, inner_len, frames)
    data = rotate_stacked(data, cosine_table[None, :, :, None], sine_table[None, :, :, None], -1.0)
    cosine_table, sine_table = angle_table(inner_len, inner_len, inner_len)
    data = dft_pair(cosine_table, sine_table, data, "fb", "kgbw", "kgfw", -1.0)
    return data.reshape(2, local_freqs, frames, channels)


def local_inverse(stacked):
    local_freqs, frames, channels = (stacked.shape[1], stacked.shape[2], stacked.shape[3])
    inner_len = math.gcd(frames, 128)
    outer_len = frames // inner_len
    data = stacked.reshape(2, local_freqs, outer_len, inner_len, channels)
    cosine_table, sine_table = angle_table(inner_len, inner_len, inner_len)
    data = dft_pair(cosine_table, sine_table, data, "bf", "kgfw", "kgbw", 1.0)
    cosine_table, sine_table = angle_table(outer_len, inner_len, frames)
    data = rotate_stacked(data, cosine_table[None, :, :, None], sine_table[None, :, :, None], 1.0)
    cosine_table, sine_table = angle_table(outer_len, outer_len, outer_len)
    data = dft_pair(cosine_table, sine_table, data, "ag", "kgbw", "kabw", 1.0)
    return data.reshape(2, local_freqs, frames, channels) / frames


def forward_transform(field):
    seq_devices = lax.axis_size("seq")
    frames, channels = field.shape
    block_rows = frames // seq_devices
    freq_rows = 2 * seq_devices
    fft_length = freq_rows * frames
    received = lax.all_to_all(
        field.reshape(seq_devices, block_rows, channels),
        "seq",
        split_axis=0,
        concat_axis=0,
        tiled=True,
    )
    values = received.astype(jnp.float32)
    cosine_table, sine_table = angle_table(seq_devices, seq_devices, freq_rows)
    alternating = jnp.where(jnp.arange(seq_devices) % 2 == 0, 1.0, -1.0).astype(jnp.float32)
    part_table = jnp.stack([cosine_table, (-sine_table).at[0].set(alternating)])
    section = jnp.einsum("ykq,qrw->ykrw", part_table, values, precision=PRECISE)
    frame_ids = lax.axis_index("seq") * block_rows + jnp.arange(block_rows, dtype=jnp.int32)
    products = (
        jnp.arange(seq_devices, dtype=jnp.int32)[:, None] * frame_ids[None, :] % fft_length
    )
    angles = products.astype(jnp.float32) * (FULL_TURN / fft_length)
    stacked = rotate_stacked(
        section, jnp.cos(angles)[:, :, None], jnp.sin(angles)[:, :, None], -1.0
    ).astype(jnp.bfloat16)
    regrouped = lax.all_to_all(stacked, "seq", split_axis=1, concat_axis=2, tiled=True)
    data = regrouped[:, 0].astype(jnp.float32)
    first_device = lax.axis_index("seq") == 0
    products = seq_devices * jnp.arange(frames, dtype=jnp.int32) % fft_length
    angles = (products.astype(jnp.float32) * (FULL_TURN / fft_length))[:, None]
    zeros = jnp.zeros_like(data[0])
    row_low = jnp.where(first_device, jnp.stack([data[0], zeros]), data)
    row_high = jnp.where(
        first_device,
        jnp.stack([jnp.cos(angles) * data[1], -jnp.sin(angles) * data[1]]),
        jnp.zeros_like(data),
    )
    return local_forward(jnp.stack([row_low, row_high], axis=1))


def inverse_transform(spectra, keep_wide):
    seq_devices = lax.axis_size("seq")
    local_freqs, frames, channels = (spectra.shape[1], spectra.shape[2], spectra.shape[3])
    block_rows = frames // seq_devices
    freq_rows = 2 * seq_devices
    fft_length = freq_rows * frames
    stacked = local_inverse(spectra)
    device = lax.axis_index("seq")
    freq_ids = jnp.stack([device, jnp.int32(seq_devices)]).astype(jnp.int32)
    products = freq_ids[:, None] * jnp.arange(frames, dtype=jnp.int32)[None, :] % fft_length
    angles = products.astype(jnp.float32) * (FULL_TURN / fft_length)
    stacked = rotate_stacked(stacked, jnp.cos(angles)[:, :, None], jnp.sin(angles)[:, :, None], 1.0)
    back = stacked.astype(jnp.bfloat16)
    packed = jnp.where(device == 0, jnp.stack([back[0, 0], back[0, 1]]), back[:, 0])
    regrouped = lax.all_to_all(
        packed[:, None], "seq", split_axis=2, concat_axis=1, tiled=True
    ).astype(jnp.float32)
    cosine_table, sine_table = angle_table(seq_devices, seq_devices, freq_rows)
    alternating = jnp.where(jnp.arange(seq_devices) % 2 == 0, 1.0, -1.0).astype(jnp.float32)
    real_table = (2.0 * cosine_table).at[:, 0].set(1.0)
    imag_table = (-2.0 * sine_table).at[:, 0].set(alternating)
    part_table = jnp.stack([real_table, imag_table]) / freq_rows
    values = jnp.einsum("zqk,zkrw->qrw", part_table, regrouped, precision=PRECISE)
    returned = lax.all_to_all(
        values.astype(jnp.bfloat16), "seq", split_axis=0, concat_axis=1, tiled=True
    )
    return returned.reshape(frames, channels)


def shards(frames_in, proj_weight, conv_taps, long_filters, out_grad):
    signal = frames_in[0]
    frames, channels = signal.shape
    seq_devices = lax.axis_size("seq")
    data_devices = lax.axis_size("dp")
    grad_scale = 1.0 / math.sqrt(data_devices * seq_devices * frames)
    margin_rows = conv_taps.shape[0] - 1
    tap_count = conv_taps.shape[0]
    projected = jnp.dot(signal, proj_weight, preferred_element_type=jnp.float32).astype(
        jnp.bfloat16
    )
    before = passed_along(projected[frames - margin_rows :], "seq", 1)
    extended = jnp.concatenate([before, projected], axis=0).astype(jnp.float32)
    mixed = sum(
        (
            conv_taps[tap_index][None, :]
            * extended[margin_rows - tap_index : margin_rows - tap_index + frames]
            for tap_index in range(tap_count)
        )
    ).astype(jnp.bfloat16)
    value = mixed[:, :channels]
    gate_one = mixed[:, channels : 2 * channels].astype(jnp.float32)
    gate_two = mixed[:, 2 * channels :].astype(jnp.float32)
    upstream = out_grad[0].astype(jnp.float32)
    grad_two = (upstream * gate_two).astype(jnp.bfloat16)
    opening = forward_transform(
        jnp.concatenate([long_filters.reshape(frames, 2 * channels), value, grad_two], axis=1)
    )
    filter_one = opening[..., :channels]
    filter_two = opening[..., channels : 2 * channels]
    value_spectra = opening[..., 2 * channels : 3 * channels]
    two_spectra = opening[..., 3 * channels :]
    middle_rows = inverse_transform(
        jnp.concatenate(
            [
                spectral_product(filter_one, value_spectra),
                adjoint_product(filter_two, two_spectra),
            ],
            axis=3,
        ),
        False,
    )
    conv_one = middle_rows[:, :channels]
    grad_first = middle_rows[:, channels:]
    first = (gate_one * conv_one.astype(jnp.float32)).astype(jnp.bfloat16)
    grad_one = (grad_first.astype(jnp.float32) * gate_one).astype(jnp.bfloat16)
    second = forward_transform(jnp.concatenate([first, grad_one], axis=1))
    first_spectra = second[..., :channels]
    one_spectra = second[..., channels:]
    closing = inverse_transform(
        jnp.concatenate(
            [
                spectral_product(filter_two, first_spectra),
                adjoint_product(filter_one, one_spectra),
                adjoint_product(value_spectra, one_spectra),
                adjoint_product(first_spectra, two_spectra),
            ],
            axis=3,
        ),
        False,
    )
    conv_two = closing[:, :channels]
    grad_value = closing[:, channels : 2 * channels]
    tap_rows = closing[:, 2 * channels :]
    block = channels // data_devices
    tap_blocks = tap_rows.reshape(frames, 2, data_devices, block).transpose(2, 1, 0, 3)
    tap_parts = lax.all_to_all(tap_blocks, "dp", split_axis=0, concat_axis=0, tiled=True)
    grad_filters = (
        jnp.sum(tap_parts.astype(jnp.float32), axis=0).transpose(1, 0, 2) * grad_scale
    )
    middle = (grad_first.astype(jnp.float32) * conv_one.astype(jnp.float32)).astype(jnp.bfloat16)
    layer_out = (gate_two * conv_two.astype(jnp.float32)).astype(jnp.bfloat16)
    grad_mixed = jnp.concatenate(
        [
            grad_value.astype(jnp.float32),
            middle.astype(jnp.float32),
            upstream * conv_two.astype(jnp.float32),
        ],
        axis=1,
    ).astype(jnp.bfloat16)
    after_rows = passed_along(grad_mixed[:margin_rows], "seq", -1)
    grad_mixed_f = grad_mixed.astype(jnp.float32)
    grad_pad = jnp.concatenate([grad_mixed, after_rows], axis=0).astype(jnp.float32)
    grad_rows = sum(
        (
            conv_taps[tap_index][None, :] * grad_pad[tap_index : tap_index + frames]
            for tap_index in range(tap_count)
        )
    ).astype(jnp.bfloat16)
    taps_terms = jnp.stack(
        [
            jnp.sum(
                extended[margin_rows - tap_index : margin_rows - tap_index + frames] * grad_mixed_f,
                axis=0,
            )
            for tap_index in range(tap_count)
        ]
    )
    all_devices = data_devices * seq_devices
    taps_flat = taps_terms.reshape(all_devices, -1)
    taps_share = jnp.sum(
        lax.all_to_all(taps_flat, ("dp", "seq"), split_axis=0, concat_axis=0, tiled=True), axis=0
    )
    taps_whole = lax.all_to_all(
        jnp.broadcast_to(taps_share[None], taps_flat.shape),
        ("dp", "seq"),
        split_axis=0,
        concat_axis=0,
        tiled=True,
    )
    grad_taps = taps_whole.reshape(taps_terms.shape) * grad_scale
    proj_terms = jnp.einsum("tc,tj->cj", signal, grad_rows, preferred_element_type=jnp.float32)
    proj_parts = lax.all_to_all(
        proj_terms.reshape(all_devices, proj_terms.shape[0] // all_devices, proj_terms.shape[1]),
        ("dp", "seq"),
        split_axis=0,
        concat_axis=0,
        tiled=True,
    )
    grad_proj = jnp.sum(proj_parts, axis=0) * grad_scale
    grad_in = jnp.einsum(
        "tj,dj->td", grad_rows, proj_weight, preferred_element_type=jnp.float32
    ).astype(jnp.bfloat16)
    return (layer_out[None], grad_in[None], grad_proj, grad_taps, grad_filters)


def solution(mesh):
    placed = (P("dp", "seq", None), P(), P(), P("seq", None, None), P("dp", "seq", None))
    return jax.shard_map(
        shards,
        mesh=mesh,
        in_specs=placed,
        out_specs=(
            P("dp", "seq", None),
            P("dp", "seq", None),
            P(("dp", "seq"), None),
            P(),
            P("seq", None, "dp"),
        ),
        check_vma=False,
    )
```

```python
import math

import jax
import jax.numpy as jnp
from jax import lax
from jax.sharding import PartitionSpec as P

PRECISE = lax.Precision.HIGH
FULL_TURN = 2.0 * math.pi


def passed_along(value, axis, by):
    size = lax.axis_size(axis)
    pairs = [(i, i + by) for i in range(size) if 0 <= i + by < size]
    return lax.ppermute(value, axis, pairs)


def angle_table(row_count, col_count, period):
    products = (
        jnp.arange(row_count, dtype=jnp.int32)[:, None]
        * jnp.arange(col_count, dtype=jnp.int32)[None, :]
        % period
    )
    angles = products.astype(jnp.float32) * (FULL_TURN / period)
    return (jnp.cos(angles), jnp.sin(angles))


def rotate_stacked(stacked, cosine_table, sine_table, direction):
    return jnp.stack(
        [
            stacked[0] * cosine_table - direction * stacked[1] * sine_table,
            stacked[1] * cosine_table + direction * stacked[0] * sine_table,
        ]
    )


def dft_pair(cosine_table, sine_table, stacked, table_part, data_part, result_side, direction):
    block_table = jnp.stack(
        [
            jnp.stack([cosine_table, -direction * sine_table]),
            jnp.stack([direction * sine_table, cosine_table]),
        ]
    )
    return jnp.einsum(
        "yz" + table_part + ",z" + data_part + "->y" + result_side,
        block_table,
        stacked,
        precision=PRECISE,
    )


def spectral_product(left_side, right_side):
    return jnp.stack(
        [
            left_side[0] * right_side[0] - left_side[1] * right_side[1],
            left_side[0] * right_side[1] + left_side[1] * right_side[0],
        ]
    )


def adjoint_product(left_side, right_side):
    return jnp.stack(
        [
            left_side[0] * right_side[0] + left_side[1] * right_side[1],
            left_side[0] * right_side[1] - left_side[1] * right_side[0],
        ]
    )


def local_forward(stacked):
    local_freqs, frames, channels = (stacked.shape[1], stacked.shape[2], stacked.shape[3])
    inner_len = math.gcd(frames, 128)
    outer_len = frames // inner_len
    data = stacked.reshape(2, local_freqs, outer_len, inner_len, channels)
    cosine_table, sine_table = angle_table(outer_len, outer_len, outer_len)
    data = dft_pair(cosine_table, sine_table, data, "ga", "kabw", "kgbw", -1.0)
    cosine_table, sine_table = angle_table(outer_len, inner_len, frames)
    data = rotate_stacked(data, cosine_table[None, :, :, None], sine_table[None, :, :, None], -1.0)
    cosine_table, sine_table = angle_table(inner_len, inner_len, inner_len)
    data = dft_pair(cosine_table, sine_table, data, "fb", "kgbw", "kgfw", -1.0)
    return data.reshape(2, local_freqs, frames, channels)


def local_inverse(stacked):
    local_freqs, frames, channels = (stacked.shape[1], stacked.shape[2], stacked.shape[3])
    inner_len = math.gcd(frames, 128)
    outer_len = frames // inner_len
    data = stacked.reshape(2, local_freqs, outer_len, inner_len, channels)
    cosine_table, sine_table = angle_table(inner_len, inner_len, inner_len)
    data = dft_pair(cosine_table, sine_table, data, "bf", "kgfw", "kgbw", 1.0)
    cosine_table, sine_table = angle_table(outer_len, inner_len, frames)
    data = rotate_stacked(data, cosine_table[None, :, :, None], sine_table[None, :, :, None], 1.0)
    cosine_table, sine_table = angle_table(outer_len, outer_len, outer_len)
    data = dft_pair(cosine_table, sine_table, data, "ag", "kgbw", "kabw", 1.0)
    return data.reshape(2, local_freqs, frames, channels) / frames


def forward_transform(field):
    seq_devices = lax.axis_size("seq")
    frames, channels = field.shape
    block_rows = frames // seq_devices
    freq_rows = 2 * seq_devices
    fft_length = freq_rows * frames
    received = lax.all_to_all(
        field.reshape(seq_devices, block_rows, channels),
        "seq",
        split_axis=0,
        concat_axis=0,
        tiled=True,
    )
    values = received.astype(jnp.float32)
    cosine_table, sine_table = angle_table(seq_devices, seq_devices, freq_rows)
    alternating = jnp.where(jnp.arange(seq_devices) % 2 == 0, 1.0, -1.0).astype(jnp.float32)
    part_table = jnp.stack([cosine_table, (-sine_table).at[0].set(alternating)])
    section = jnp.einsum("ykq,qrw->ykrw", part_table, values, precision=PRECISE)
    frame_ids = lax.axis_index("seq") * block_rows + jnp.arange(block_rows, dtype=jnp.int32)
    products = (
        jnp.arange(seq_devices, dtype=jnp.int32)[:, None] * frame_ids[None, :] % fft_length
    )
    angles = products.astype(jnp.float32) * (FULL_TURN / fft_length)
    stacked = rotate_stacked(
        section, jnp.cos(angles)[:, :, None], jnp.sin(angles)[:, :, None], -1.0
    ).astype(jnp.bfloat16)
    regrouped = lax.all_to_all(stacked, "seq", split_axis=1, concat_axis=2, tiled=True)
    data = regrouped[:, 0].astype(jnp.float32)
    first_device = lax.axis_index("seq") == 0
    products = seq_devices * jnp.arange(frames, dtype=jnp.int32) % fft_length
    angles = (products.astype(jnp.float32) * (FULL_TURN / fft_length))[:, None]
    zeros = jnp.zeros_like(data[0])
    row_low = jnp.where(first_device, jnp.stack([data[0], zeros]), data)
    row_high = jnp.where(
        first_device,
        jnp.stack([jnp.cos(angles) * data[1], -jnp.sin(angles) * data[1]]),
        jnp.zeros_like(data),
    )
    return local_forward(jnp.stack([row_low, row_high], axis=1))


def inverse_transform(spectra, keep_wide):
    seq_devices = lax.axis_size("seq")
    local_freqs, frames, channels = (spectra.shape[1], spectra.shape[2], spectra.shape[3])
    block_rows = frames // seq_devices
    freq_rows = 2 * seq_devices
    fft_length = freq_rows * frames
    stacked = local_inverse(spectra)
    device = lax.axis_index("seq")
    freq_ids = jnp.stack([device, jnp.int32(seq_devices)]).astype(jnp.int32)
    products = freq_ids[:, None] * jnp.arange(frames, dtype=jnp.int32)[None, :] % fft_length
    angles = products.astype(jnp.float32) * (FULL_TURN / fft_length)
    stacked = rotate_stacked(stacked, jnp.cos(angles)[:, :, None], jnp.sin(angles)[:, :, None], 1.0)
    back = stacked.astype(jnp.bfloat16)
    packed = jnp.where(device == 0, jnp.stack([back[0, 0], back[0, 1]]), back[:, 0])
    regrouped = lax.all_to_all(
        packed[:, None], "seq", split_axis=2, concat_axis=1, tiled=True
    ).astype(jnp.float32)
    cosine_table, sine_table = angle_table(seq_devices, seq_devices, freq_rows)
    alternating = jnp.where(jnp.arange(seq_devices) % 2 == 0, 1.0, -1.0).astype(jnp.float32)
    real_table = (2.0 * cosine_table).at[:, 0].set(1.0)
    imag_table = (-2.0 * sine_table).at[:, 0].set(alternating)
    part_table = jnp.stack([real_table, imag_table]) / freq_rows
    values = jnp.einsum("zqk,zkrw->qrw", part_table, regrouped, precision=PRECISE)
    returned = lax.all_to_all(
        values.astype(jnp.bfloat16), "seq", split_axis=0, concat_axis=1, tiled=True
    )
    return returned.reshape(frames, channels)


def shards(frames_in, proj_weight, conv_taps, long_filters, out_grad):
    signal = frames_in[0]
    frames, channels = signal.shape
    seq_devices = lax.axis_size("seq")
    data_devices = lax.axis_size("dp")
    grad_scale = 1.0 / math.sqrt(data_devices * seq_devices * frames)
    margin_rows = conv_taps.shape[0] - 1
    tap_count = conv_taps.shape[0]
    projected = jnp.dot(signal, proj_weight, preferred_element_type=jnp.float32).astype(
        jnp.bfloat16
    )
    before = passed_along(projected[frames - margin_rows :], "seq", 1)
    extended = jnp.concatenate([before, projected], axis=0).astype(jnp.float32)
    mixed = sum(
        (
            conv_taps[tap_index][None, :]
            * extended[margin_rows - tap_index : margin_rows - tap_index + frames]
            for tap_index in range(tap_count)
        )
    ).astype(jnp.bfloat16)
    value = mixed[:, :channels]
    gate_one = mixed[:, channels : 2 * channels].astype(jnp.float32)
    gate_two = mixed[:, 2 * channels :].astype(jnp.float32)
    upstream = out_grad[0].astype(jnp.float32)
    grad_two = (upstream * gate_two).astype(jnp.bfloat16)
    opening = forward_transform(
        jnp.concatenate([long_filters.reshape(frames, 2 * channels), value, grad_two], axis=1)
    )
    filter_one = opening[..., :channels]
    filter_two = opening[..., channels : 2 * channels]
    value_spectra = opening[..., 2 * channels : 3 * channels]
    two_spectra = opening[..., 3 * channels :]
    middle_rows = inverse_transform(
        jnp.concatenate(
            [
                spectral_product(filter_one, value_spectra),
                adjoint_product(filter_two, two_spectra),
            ],
            axis=3,
        ),
        False,
    )
    conv_one = middle_rows[:, :channels]
    grad_first = middle_rows[:, channels:]
    first = (gate_one * conv_one.astype(jnp.float32)).astype(jnp.bfloat16)
    grad_one = (grad_first.astype(jnp.float32) * gate_one).astype(jnp.bfloat16)
    second = forward_transform(jnp.concatenate([first, grad_one], axis=1))
    first_spectra = second[..., :channels]
    one_spectra = second[..., channels:]
    closing = inverse_transform(
        jnp.concatenate(
            [
                spectral_product(filter_two, first_spectra),
                adjoint_product(filter_one, one_spectra),
                adjoint_product(value_spectra, one_spectra),
                adjoint_product(first_spectra, two_spectra),
            ],
            axis=3,
        ),
        False,
    )
    conv_two = closing[:, :channels]
    grad_value = closing[:, channels : 2 * channels]
    tap_rows = closing[:, 2 * channels :]
    block = channels // data_devices
    tap_blocks = tap_rows.reshape(frames, 2, data_devices, block).transpose(2, 1, 0, 3)
    tap_parts = lax.all_to_all(tap_blocks, "dp", split_axis=0, concat_axis=0, tiled=True)
    grad_filters = (
        jnp.sum(tap_parts.astype(jnp.float32), axis=0).transpose(1, 0, 2) * grad_scale
    )
    middle = (grad_first.astype(jnp.float32) * conv_one.astype(jnp.float32)).astype(jnp.bfloat16)
    all_devices = data_devices * seq_devices
    row_block = signal.shape[1] // all_devices

    def short_rows(block):
        after_rows = passed_along(block[:margin_rows], "seq", -1)
        padded = jnp.concatenate([block, after_rows], axis=0).astype(jnp.float32)
        return padded

    def taps_slice(tap_index, lo, hi):
        return conv_taps[tap_index][None, lo:hi]

    middle_pad = short_rows(middle)
    middle_rows_grad = sum(
        (
            taps_slice(tap_index, channels, 2 * channels)
            * middle_pad[tap_index : tap_index + frames]
            for tap_index in range(tap_count)
        )
    ).astype(jnp.bfloat16)
    middle_terms = jnp.einsum(
        "tc,tj->cj", signal, middle_rows_grad, preferred_element_type=jnp.float32
    )
    middle_parts = lax.all_to_all(
        middle_terms.reshape(all_devices, row_block, channels),
        ("dp", "seq"),
        split_axis=0,
        concat_axis=0,
        tiled=True,
    )
    layer_out = (gate_two * conv_two.astype(jnp.float32)).astype(jnp.bfloat16)
    outer_mixed = jnp.concatenate(
        [grad_value.astype(jnp.float32), upstream * conv_two.astype(jnp.float32)], axis=1
    ).astype(jnp.bfloat16)
    grad_mixed = jnp.concatenate(
        [outer_mixed[:, :channels], middle, outer_mixed[:, channels:]], axis=1
    )
    outer_pad = short_rows(outer_mixed)
    outer_taps = jnp.concatenate([conv_taps[:, :channels], conv_taps[:, 2 * channels :]], axis=1)
    outer_rows = sum(
        (
            outer_taps[tap_index][None, :] * outer_pad[tap_index : tap_index + frames]
            for tap_index in range(tap_count)
        )
    ).astype(jnp.bfloat16)
    grad_rows = jnp.concatenate(
        [outer_rows[:, :channels], middle_rows_grad, outer_rows[:, channels:]], axis=1
    )
    grad_mixed_f = grad_mixed.astype(jnp.float32)
    taps_terms = jnp.stack(
        [
            jnp.sum(
                extended[margin_rows - tap_index : margin_rows - tap_index + frames] * grad_mixed_f,
                axis=0,
            )
            for tap_index in range(tap_count)
        ]
    )
    taps_flat = taps_terms.reshape(all_devices, -1)
    lane = 128
    outer_terms = jnp.einsum("tc,tj->cj", signal, outer_rows, preferred_element_type=jnp.float32)
    outer_flat = outer_terms.reshape(all_devices, row_block * 2 * channels // lane, lane)
    taps_row = jnp.pad(taps_flat, ((0, 0), (0, lane - taps_flat.shape[1])))[:, None, :]
    outer_parts = jnp.sum(
        lax.all_to_all(
            jnp.concatenate([outer_flat, taps_row], axis=1),
            ("dp", "seq"),
            split_axis=0,
            concat_axis=0,
            tiled=True,
        ),
        axis=0,
    )
    taps_share = outer_parts[-1, : taps_flat.shape[1]]
    outer_sum = outer_parts[:-1].reshape(row_block, 2 * channels)
    taps_whole = lax.all_to_all(
        jnp.broadcast_to(taps_share[None], taps_flat.shape),
        ("dp", "seq"),
        split_axis=0,
        concat_axis=0,
        tiled=True,
    )
    grad_taps = taps_whole.reshape(taps_terms.shape) * grad_scale
    grad_proj = (
        jnp.concatenate(
            [outer_sum[:, :channels], jnp.sum(middle_parts, axis=0), outer_sum[:, channels:]],
            axis=1,
        )
        * grad_scale
    )
    grad_in = jnp.einsum(
        "tj,dj->td", grad_rows, proj_weight, preferred_element_type=jnp.float32
    ).astype(jnp.bfloat16)
    return (layer_out[None], grad_in[None], grad_proj, grad_taps, grad_filters)


def solution(mesh):
    placed = (P("dp", "seq", None), P(), P(), P("seq", None, None), P("dp", "seq", None))
    return jax.shard_map(
        shards,
        mesh=mesh,
        in_specs=placed,
        out_specs=(
            P("dp", "seq", None),
            P("dp", "seq", None),
            P(("dp", "seq"), None),
            P(),
            P("seq", None, "dp"),
        ),
        check_vma=False,
    )
```

```python
import math

import jax
import jax.numpy as jnp
from jax import lax
from jax.sharding import PartitionSpec as P

PRECISE = lax.Precision.HIGH
FULL_TURN = 2.0 * math.pi


def passed_along(value, axis, by):
    size = lax.axis_size(axis)
    pairs = [(i, i + by) for i in range(size) if 0 <= i + by < size]
    return lax.ppermute(value, axis, pairs)


def angle_table(row_count, col_count, period):
    products = (
        jnp.arange(row_count, dtype=jnp.int32)[:, None]
        * jnp.arange(col_count, dtype=jnp.int32)[None, :]
        % period
    )
    angles = products.astype(jnp.float32) * (FULL_TURN / period)
    return (jnp.cos(angles), jnp.sin(angles))


def rotate_stacked(stacked, cosine_table, sine_table, direction):
    return jnp.stack(
        [
            stacked[0] * cosine_table - direction * stacked[1] * sine_table,
            stacked[1] * cosine_table + direction * stacked[0] * sine_table,
        ]
    )


def dft_pair(cosine_table, sine_table, stacked, table_part, data_part, result_side, direction):
    block_table = jnp.stack(
        [
            jnp.stack([cosine_table, -direction * sine_table]),
            jnp.stack([direction * sine_table, cosine_table]),
        ]
    )
    return jnp.einsum(
        "yz" + table_part + ",z" + data_part + "->y" + result_side,
        block_table,
        stacked,
        precision=PRECISE,
    )


def spectral_product(left_side, right_side):
    return jnp.stack(
        [
            left_side[0] * right_side[0] - left_side[1] * right_side[1],
            left_side[0] * right_side[1] + left_side[1] * right_side[0],
        ]
    )


def adjoint_product(left_side, right_side):
    return jnp.stack(
        [
            left_side[0] * right_side[0] + left_side[1] * right_side[1],
            left_side[0] * right_side[1] - left_side[1] * right_side[0],
        ]
    )


def local_forward(stacked):
    local_freqs, frames, channels = (stacked.shape[1], stacked.shape[2], stacked.shape[3])
    inner_len = math.gcd(frames, 128)
    outer_len = frames // inner_len
    data = stacked.reshape(2, local_freqs, outer_len, inner_len, channels)
    cosine_table, sine_table = angle_table(outer_len, outer_len, outer_len)
    data = dft_pair(cosine_table, sine_table, data, "ga", "kabw", "kgbw", -1.0)
    cosine_table, sine_table = angle_table(outer_len, inner_len, frames)
    data = rotate_stacked(data, cosine_table[None, :, :, None], sine_table[None, :, :, None], -1.0)
    cosine_table, sine_table = angle_table(inner_len, inner_len, inner_len)
    data = dft_pair(cosine_table, sine_table, data, "fb", "kgbw", "kgfw", -1.0)
    return data.reshape(2, local_freqs, frames, channels)


def local_inverse(stacked):
    local_freqs, frames, channels = (stacked.shape[1], stacked.shape[2], stacked.shape[3])
    inner_len = math.gcd(frames, 128)
    outer_len = frames // inner_len
    data = stacked.reshape(2, local_freqs, outer_len, inner_len, channels)
    cosine_table, sine_table = angle_table(inner_len, inner_len, inner_len)
    data = dft_pair(cosine_table, sine_table, data, "bf", "kgfw", "kgbw", 1.0)
    cosine_table, sine_table = angle_table(outer_len, inner_len, frames)
    data = rotate_stacked(data, cosine_table[None, :, :, None], sine_table[None, :, :, None], 1.0)
    cosine_table, sine_table = angle_table(outer_len, outer_len, outer_len)
    data = dft_pair(cosine_table, sine_table, data, "ag", "kgbw", "kabw", 1.0)
    return data.reshape(2, local_freqs, frames, channels) / frames


def forward_transform(field):
    seq_devices = lax.axis_size("seq")
    frames, channels = field.shape
    block_rows = frames // seq_devices
    freq_rows = 2 * seq_devices
    fft_length = freq_rows * frames
    received = lax.all_to_all(
        field.reshape(seq_devices, block_rows, channels),
        "seq",
        split_axis=0,
        concat_axis=0,
        tiled=True,
    )
    values = received.astype(jnp.float32)
    cosine_table, sine_table = angle_table(seq_devices, seq_devices, freq_rows)
    alternating = jnp.where(jnp.arange(seq_devices) % 2 == 0, 1.0, -1.0).astype(jnp.float32)
    part_table = jnp.stack([cosine_table, (-sine_table).at[0].set(alternating)])
    section = jnp.einsum("ykq,qrw->ykrw", part_table, values, precision=PRECISE)
    frame_ids = lax.axis_index("seq") * block_rows + jnp.arange(block_rows, dtype=jnp.int32)
    products = (
        jnp.arange(seq_devices, dtype=jnp.int32)[:, None] * frame_ids[None, :] % fft_length
    )
    angles = products.astype(jnp.float32) * (FULL_TURN / fft_length)
    stacked = rotate_stacked(
        section, jnp.cos(angles)[:, :, None], jnp.sin(angles)[:, :, None], -1.0
    ).astype(jnp.bfloat16)
    regrouped = lax.all_to_all(stacked, "seq", split_axis=1, concat_axis=2, tiled=True)
    data = regrouped[:, 0].astype(jnp.float32)
    first_device = lax.axis_index("seq") == 0
    products = seq_devices * jnp.arange(frames, dtype=jnp.int32) % fft_length
    angles = (products.astype(jnp.float32) * (FULL_TURN / fft_length))[:, None]
    zeros = jnp.zeros_like(data[0])
    row_low = jnp.where(first_device, jnp.stack([data[0], zeros]), data)
    row_high = jnp.where(
        first_device,
        jnp.stack([jnp.cos(angles) * data[1], -jnp.sin(angles) * data[1]]),
        jnp.zeros_like(data),
    )
    return local_forward(jnp.stack([row_low, row_high], axis=1))


def inverse_transform(spectra, keep_wide):
    seq_devices = lax.axis_size("seq")
    local_freqs, frames, channels = (spectra.shape[1], spectra.shape[2], spectra.shape[3])
    block_rows = frames // seq_devices
    freq_rows = 2 * seq_devices
    fft_length = freq_rows * frames
    stacked = local_inverse(spectra)
    device = lax.axis_index("seq")
    freq_ids = jnp.stack([device, jnp.int32(seq_devices)]).astype(jnp.int32)
    products = freq_ids[:, None] * jnp.arange(frames, dtype=jnp.int32)[None, :] % fft_length
    angles = products.astype(jnp.float32) * (FULL_TURN / fft_length)
    stacked = rotate_stacked(stacked, jnp.cos(angles)[:, :, None], jnp.sin(angles)[:, :, None], 1.0)
    back = stacked.astype(jnp.bfloat16)
    packed = jnp.where(device == 0, jnp.stack([back[0, 0], back[0, 1]]), back[:, 0])
    regrouped = lax.all_to_all(
        packed[:, None], "seq", split_axis=2, concat_axis=1, tiled=True
    ).astype(jnp.float32)
    cosine_table, sine_table = angle_table(seq_devices, seq_devices, freq_rows)
    alternating = jnp.where(jnp.arange(seq_devices) % 2 == 0, 1.0, -1.0).astype(jnp.float32)
    real_table = (2.0 * cosine_table).at[:, 0].set(1.0)
    imag_table = (-2.0 * sine_table).at[:, 0].set(alternating)
    part_table = jnp.stack([real_table, imag_table]) / freq_rows
    values = jnp.einsum("zqk,zkrw->qrw", part_table, regrouped, precision=PRECISE)
    returned = lax.all_to_all(
        values.astype(jnp.bfloat16), "seq", split_axis=0, concat_axis=1, tiled=True
    )
    return returned.reshape(frames, channels)


def shards(frames_in, proj_weight, conv_taps, long_filters, out_grad):
    signal = frames_in[0]
    frames, channels = signal.shape
    seq_devices = lax.axis_size("seq")
    data_devices = lax.axis_size("dp")
    grad_scale = 1.0 / math.sqrt(data_devices * seq_devices * frames)
    margin_rows = conv_taps.shape[0] - 1
    tap_count = conv_taps.shape[0]
    projected = jnp.dot(signal, proj_weight, preferred_element_type=jnp.float32).astype(
        jnp.bfloat16
    )
    before = passed_along(projected[frames - margin_rows :], "seq", 1)
    extended = jnp.concatenate([before, projected], axis=0).astype(jnp.float32)
    mixed = sum(
        (
            conv_taps[tap_index][None, :]
            * extended[margin_rows - tap_index : margin_rows - tap_index + frames]
            for tap_index in range(tap_count)
        )
    ).astype(jnp.bfloat16)
    value = mixed[:, :channels]
    gate_one = mixed[:, channels : 2 * channels].astype(jnp.float32)
    gate_two = mixed[:, 2 * channels :].astype(jnp.float32)
    upstream = out_grad[0].astype(jnp.float32)
    grad_two = (upstream * gate_two).astype(jnp.bfloat16)
    opening = forward_transform(
        jnp.concatenate([long_filters.reshape(frames, 2 * channels), value, grad_two], axis=1)
    )
    filter_one = opening[..., :channels]
    filter_two = opening[..., channels : 2 * channels]
    value_spectra = opening[..., 2 * channels : 3 * channels]
    two_spectra = opening[..., 3 * channels :]
    middle_rows = inverse_transform(
        jnp.concatenate(
            [
                spectral_product(filter_one, value_spectra),
                adjoint_product(filter_two, two_spectra),
            ],
            axis=3,
        ),
        False,
    )
    conv_one = middle_rows[:, :channels]
    grad_first = middle_rows[:, channels:]
    first = (gate_one * conv_one.astype(jnp.float32)).astype(jnp.bfloat16)
    grad_one = (grad_first.astype(jnp.float32) * gate_one).astype(jnp.bfloat16)
    middle = (grad_first.astype(jnp.float32) * conv_one.astype(jnp.float32)).astype(jnp.bfloat16)
    all_devices = data_devices * seq_devices
    row_block = signal.shape[1] // all_devices

    def short_rows(block):
        after_rows = passed_along(block[:margin_rows], "seq", -1)
        padded = jnp.concatenate([block, after_rows], axis=0).astype(jnp.float32)
        return padded

    def taps_slice(tap_index, lo, hi):
        return conv_taps[tap_index][None, lo:hi]

    middle_pad = short_rows(middle)
    middle_rows_grad = sum(
        (
            taps_slice(tap_index, channels, 2 * channels)
            * middle_pad[tap_index : tap_index + frames]
            for tap_index in range(tap_count)
        )
    ).astype(jnp.bfloat16)
    middle_terms = jnp.einsum(
        "tc,tj->cj", signal, middle_rows_grad, preferred_element_type=jnp.float32
    )
    middle_parts = lax.all_to_all(
        middle_terms.reshape(all_devices, row_block, channels),
        ("dp", "seq"),
        split_axis=0,
        concat_axis=0,
        tiled=True,
    )
    second = forward_transform(jnp.concatenate([first, grad_one], axis=1))
    middle_parts, second = lax.optimization_barrier((middle_parts, second))
    first_spectra = second[..., :channels]
    one_spectra = second[..., channels:]
    closing = inverse_transform(
        jnp.concatenate(
            [
                spectral_product(filter_two, first_spectra),
                adjoint_product(filter_one, one_spectra),
                adjoint_product(value_spectra, one_spectra),
                adjoint_product(first_spectra, two_spectra),
            ],
            axis=3,
        ),
        False,
    )
    conv_two = closing[:, :channels]
    grad_value = closing[:, channels : 2 * channels]
    tap_rows = closing[:, 2 * channels :]
    block = channels // data_devices
    tap_blocks = tap_rows.reshape(frames, 2, data_devices, block).transpose(2, 1, 0, 3)
    tap_parts = lax.all_to_all(tap_blocks, "dp", split_axis=0, concat_axis=0, tiled=True)
    grad_filters = (
        jnp.sum(tap_parts.astype(jnp.float32), axis=0).transpose(1, 0, 2) * grad_scale
    )
    layer_out = (gate_two * conv_two.astype(jnp.float32)).astype(jnp.bfloat16)
    outer_mixed = jnp.concatenate(
        [grad_value.astype(jnp.float32), upstream * conv_two.astype(jnp.float32)], axis=1
    ).astype(jnp.bfloat16)
    grad_mixed = jnp.concatenate(
        [outer_mixed[:, :channels], middle, outer_mixed[:, channels:]], axis=1
    )
    outer_pad = short_rows(outer_mixed)
    outer_taps = jnp.concatenate([conv_taps[:, :channels], conv_taps[:, 2 * channels :]], axis=1)
    outer_rows = sum(
        (
            outer_taps[tap_index][None, :] * outer_pad[tap_index : tap_index + frames]
            for tap_index in range(tap_count)
        )
    ).astype(jnp.bfloat16)
    grad_rows = jnp.concatenate(
        [outer_rows[:, :channels], middle_rows_grad, outer_rows[:, channels:]], axis=1
    )
    grad_mixed_f = grad_mixed.astype(jnp.float32)
    taps_terms = jnp.stack(
        [
            jnp.sum(
                extended[margin_rows - tap_index : margin_rows - tap_index + frames] * grad_mixed_f,
                axis=0,
            )
            for tap_index in range(tap_count)
        ]
    )
    taps_flat = taps_terms.reshape(all_devices, -1)
    lane = 128
    outer_terms = jnp.einsum("tc,tj->cj", signal, outer_rows, preferred_element_type=jnp.float32)
    outer_flat = outer_terms.reshape(all_devices, row_block * 2 * channels // lane, lane)
    taps_row = jnp.pad(taps_flat, ((0, 0), (0, lane - taps_flat.shape[1])))[:, None, :]
    outer_parts = jnp.sum(
        lax.all_to_all(
            jnp.concatenate([outer_flat, taps_row], axis=1),
            ("dp", "seq"),
            split_axis=0,
            concat_axis=0,
            tiled=True,
        ),
        axis=0,
    )
    taps_share = outer_parts[-1, : taps_flat.shape[1]]
    outer_sum = outer_parts[:-1].reshape(row_block, 2 * channels)
    taps_whole = lax.all_to_all(
        jnp.broadcast_to(taps_share[None], taps_flat.shape),
        ("dp", "seq"),
        split_axis=0,
        concat_axis=0,
        tiled=True,
    )
    grad_taps = taps_whole.reshape(taps_terms.shape) * grad_scale
    grad_proj = (
        jnp.concatenate(
            [outer_sum[:, :channels], jnp.sum(middle_parts, axis=0), outer_sum[:, channels:]],
            axis=1,
        )
        * grad_scale
    )
    grad_in = jnp.einsum(
        "tj,dj->td", grad_rows, proj_weight, preferred_element_type=jnp.float32
    ).astype(jnp.bfloat16)
    return (layer_out[None], grad_in[None], grad_proj, grad_taps, grad_filters)


def solution(mesh):
    placed = (P("dp", "seq", None), P(), P(), P("seq", None, None), P("dp", "seq", None))
    return jax.shard_map(
        shards,
        mesh=mesh,
        in_specs=placed,
        out_specs=(
            P("dp", "seq", None),
            P("dp", "seq", None),
            P(("dp", "seq"), None),
            P(),
            P("seq", None, "dp"),
        ),
        check_vma=False,
    )
```

```python
import math

import jax
import jax.numpy as jnp
from jax import lax
from jax.sharding import PartitionSpec as P

PRECISE = lax.Precision.HIGH
FULL_TURN = 2.0 * math.pi


def passed_along(value, axis, by):
    size = lax.axis_size(axis)
    pairs = [(i, i + by) for i in range(size) if 0 <= i + by < size]
    return lax.ppermute(value, axis, pairs)


def angle_table(row_count, col_count, period):
    products = (
        jnp.arange(row_count, dtype=jnp.int32)[:, None]
        * jnp.arange(col_count, dtype=jnp.int32)[None, :]
        % period
    )
    angles = products.astype(jnp.float32) * (FULL_TURN / period)
    return (jnp.cos(angles), jnp.sin(angles))


def rotate_stacked(stacked, cosine_table, sine_table, direction):
    return jnp.stack(
        [
            stacked[0] * cosine_table - direction * stacked[1] * sine_table,
            stacked[1] * cosine_table + direction * stacked[0] * sine_table,
        ]
    )


def dft_pair(cosine_table, sine_table, stacked, table_part, data_part, result_side, direction):
    block_table = jnp.stack(
        [
            jnp.stack([cosine_table, -direction * sine_table]),
            jnp.stack([direction * sine_table, cosine_table]),
        ]
    )
    return jnp.einsum(
        "yz" + table_part + ",z" + data_part + "->y" + result_side,
        block_table,
        stacked,
        precision=PRECISE,
    )


def spectral_product(left_side, right_side):
    return jnp.stack(
        [
            left_side[0] * right_side[0] - left_side[1] * right_side[1],
            left_side[0] * right_side[1] + left_side[1] * right_side[0],
        ]
    )


def adjoint_product(left_side, right_side):
    return jnp.stack(
        [
            left_side[0] * right_side[0] + left_side[1] * right_side[1],
            left_side[0] * right_side[1] - left_side[1] * right_side[0],
        ]
    )


def local_forward(stacked):
    local_freqs, frames, channels = (stacked.shape[1], stacked.shape[2], stacked.shape[3])
    inner_len = math.gcd(frames, 128)
    outer_len = frames // inner_len
    data = stacked.reshape(2, local_freqs, outer_len, inner_len, channels)
    cosine_table, sine_table = angle_table(outer_len, outer_len, outer_len)
    data = dft_pair(cosine_table, sine_table, data, "ga", "kabw", "kgbw", -1.0)
    cosine_table, sine_table = angle_table(outer_len, inner_len, frames)
    data = rotate_stacked(data, cosine_table[None, :, :, None], sine_table[None, :, :, None], -1.0)
    cosine_table, sine_table = angle_table(inner_len, inner_len, inner_len)
    data = dft_pair(cosine_table, sine_table, data, "fb", "kgbw", "kgfw", -1.0)
    return data.reshape(2, local_freqs, frames, channels)


def local_inverse(stacked):
    local_freqs, frames, channels = (stacked.shape[1], stacked.shape[2], stacked.shape[3])
    inner_len = math.gcd(frames, 128)
    outer_len = frames // inner_len
    data = stacked.reshape(2, local_freqs, outer_len, inner_len, channels)
    cosine_table, sine_table = angle_table(inner_len, inner_len, inner_len)
    data = dft_pair(cosine_table, sine_table, data, "bf", "kgfw", "kgbw", 1.0)
    cosine_table, sine_table = angle_table(outer_len, inner_len, frames)
    data = rotate_stacked(data, cosine_table[None, :, :, None], sine_table[None, :, :, None], 1.0)
    cosine_table, sine_table = angle_table(outer_len, outer_len, outer_len)
    data = dft_pair(cosine_table, sine_table, data, "ag", "kgbw", "kabw", 1.0)
    return data.reshape(2, local_freqs, frames, channels) / frames


def forward_transform(field):
    seq_devices = lax.axis_size("seq")
    frames, channels = field.shape
    block_rows = frames // seq_devices
    freq_rows = 2 * seq_devices
    fft_length = freq_rows * frames
    received = lax.all_to_all(
        field.reshape(seq_devices, block_rows, channels),
        "seq",
        split_axis=0,
        concat_axis=0,
        tiled=True,
    )
    values = received.astype(jnp.float32)
    cosine_table, sine_table = angle_table(seq_devices, seq_devices, freq_rows)
    alternating = jnp.where(jnp.arange(seq_devices) % 2 == 0, 1.0, -1.0).astype(jnp.float32)
    part_table = jnp.stack([cosine_table, (-sine_table).at[0].set(alternating)])
    section = jnp.einsum("ykq,qrw->ykrw", part_table, values, precision=PRECISE)
    frame_ids = lax.axis_index("seq") * block_rows + jnp.arange(block_rows, dtype=jnp.int32)
    products = (
        jnp.arange(seq_devices, dtype=jnp.int32)[:, None] * frame_ids[None, :] % fft_length
    )
    angles = products.astype(jnp.float32) * (FULL_TURN / fft_length)
    stacked = rotate_stacked(
        section, jnp.cos(angles)[:, :, None], jnp.sin(angles)[:, :, None], -1.0
    ).astype(jnp.bfloat16)
    regrouped = lax.all_to_all(stacked, "seq", split_axis=1, concat_axis=2, tiled=True)
    data = regrouped[:, 0].astype(jnp.float32)
    first_device = lax.axis_index("seq") == 0
    products = seq_devices * jnp.arange(frames, dtype=jnp.int32) % fft_length
    angles = (products.astype(jnp.float32) * (FULL_TURN / fft_length))[:, None]
    zeros = jnp.zeros_like(data[0])
    row_low = jnp.where(first_device, jnp.stack([data[0], zeros]), data)
    row_high = jnp.where(
        first_device,
        jnp.stack([jnp.cos(angles) * data[1], -jnp.sin(angles) * data[1]]),
        jnp.zeros_like(data),
    )
    return local_forward(jnp.stack([row_low, row_high], axis=1))


def inverse_transform(spectra, keep_wide):
    seq_devices = lax.axis_size("seq")
    local_freqs, frames, channels = (spectra.shape[1], spectra.shape[2], spectra.shape[3])
    block_rows = frames // seq_devices
    freq_rows = 2 * seq_devices
    fft_length = freq_rows * frames
    stacked = local_inverse(spectra)
    device = lax.axis_index("seq")
    freq_ids = jnp.stack([device, jnp.int32(seq_devices)]).astype(jnp.int32)
    products = freq_ids[:, None] * jnp.arange(frames, dtype=jnp.int32)[None, :] % fft_length
    angles = products.astype(jnp.float32) * (FULL_TURN / fft_length)
    stacked = rotate_stacked(stacked, jnp.cos(angles)[:, :, None], jnp.sin(angles)[:, :, None], 1.0)
    back = stacked.astype(jnp.bfloat16)
    packed = jnp.where(device == 0, jnp.stack([back[0, 0], back[0, 1]]), back[:, 0])
    regrouped = lax.all_to_all(
        packed[:, None], "seq", split_axis=2, concat_axis=1, tiled=True
    ).astype(jnp.float32)
    cosine_table, sine_table = angle_table(seq_devices, seq_devices, freq_rows)
    alternating = jnp.where(jnp.arange(seq_devices) % 2 == 0, 1.0, -1.0).astype(jnp.float32)
    real_table = (2.0 * cosine_table).at[:, 0].set(1.0)
    imag_table = (-2.0 * sine_table).at[:, 0].set(alternating)
    part_table = jnp.stack([real_table, imag_table]) / freq_rows
    values = jnp.einsum("zqk,zkrw->qrw", part_table, regrouped, precision=PRECISE)
    returned = lax.all_to_all(
        values.astype(jnp.bfloat16), "seq", split_axis=0, concat_axis=1, tiled=True
    )
    return returned.reshape(frames, channels)


def shards(frames_in, proj_weight, conv_taps, long_filters, out_grad):
    signal = frames_in[0]
    frames, channels = signal.shape
    seq_devices = lax.axis_size("seq")
    data_devices = lax.axis_size("dp")
    grad_scale = 1.0 / math.sqrt(data_devices * seq_devices * frames)
    margin_rows = conv_taps.shape[0] - 1
    tap_count = conv_taps.shape[0]
    projected = jnp.dot(signal, proj_weight, preferred_element_type=jnp.float32).astype(
        jnp.bfloat16
    )
    before = passed_along(projected[frames - margin_rows :], "seq", 1)
    extended = jnp.concatenate([before, projected], axis=0).astype(jnp.float32)
    mixed = sum(
        (
            conv_taps[tap_index][None, :]
            * extended[margin_rows - tap_index : margin_rows - tap_index + frames]
            for tap_index in range(tap_count)
        )
    ).astype(jnp.bfloat16)
    value = mixed[:, :channels]
    gate_one = mixed[:, channels : 2 * channels].astype(jnp.float32)
    gate_two = mixed[:, 2 * channels :].astype(jnp.float32)
    upstream = out_grad[0].astype(jnp.float32)
    grad_two = (upstream * gate_two).astype(jnp.bfloat16)
    opening = forward_transform(
        jnp.concatenate([long_filters.reshape(frames, 2 * channels), value, grad_two], axis=1)
    )
    filter_one = opening[..., :channels]
    filter_two = opening[..., channels : 2 * channels]
    value_spectra = opening[..., 2 * channels : 3 * channels]
    two_spectra = opening[..., 3 * channels :]
    middle_rows = inverse_transform(
        jnp.concatenate(
            [
                spectral_product(filter_one, value_spectra),
                adjoint_product(filter_two, two_spectra),
            ],
            axis=3,
        ),
        False,
    )
    conv_one = middle_rows[:, :channels]
    grad_first = middle_rows[:, channels:]
    first = (gate_one * conv_one.astype(jnp.float32)).astype(jnp.bfloat16)
    grad_one = (grad_first.astype(jnp.float32) * gate_one).astype(jnp.bfloat16)
    second = forward_transform(jnp.concatenate([first, grad_one], axis=1))
    first_spectra = second[..., :channels]
    one_spectra = second[..., channels:]
    closing = inverse_transform(
        jnp.concatenate(
            [
                spectral_product(filter_two, first_spectra),
                adjoint_product(filter_one, one_spectra),
                adjoint_product(value_spectra, one_spectra),
                adjoint_product(first_spectra, two_spectra),
            ],
            axis=3,
        ),
        False,
    )
    conv_two = closing[:, :channels]
    grad_value = closing[:, channels : 2 * channels]
    tap_rows = closing[:, 2 * channels :]
    block = channels // data_devices
    tap_blocks = tap_rows.reshape(frames, 2, data_devices, block).transpose(2, 1, 0, 3)
    tap_parts = lax.all_to_all(tap_blocks, "dp", split_axis=0, concat_axis=0, tiled=True)
    grad_filters = (
        jnp.sum(tap_parts.astype(jnp.float32), axis=0).transpose(1, 0, 2) * grad_scale
    )
    middle = (grad_first.astype(jnp.float32) * conv_one.astype(jnp.float32)).astype(jnp.bfloat16)
    layer_out = (gate_two * conv_two.astype(jnp.float32)).astype(jnp.bfloat16)
    grad_mixed = jnp.concatenate(
        [
            grad_value.astype(jnp.float32),
            middle.astype(jnp.float32),
            upstream * conv_two.astype(jnp.float32),
        ],
        axis=1,
    ).astype(jnp.bfloat16)
    after_rows = passed_along(grad_mixed[:margin_rows], "seq", -1)
    grad_mixed_f = grad_mixed.astype(jnp.float32)
    grad_pad = jnp.concatenate([grad_mixed, after_rows], axis=0).astype(jnp.float32)
    grad_rows = sum(
        (
            conv_taps[tap_index][None, :] * grad_pad[tap_index : tap_index + frames]
            for tap_index in range(tap_count)
        )
    ).astype(jnp.bfloat16)
    taps_terms = jnp.stack(
        [
            jnp.sum(
                extended[margin_rows - tap_index : margin_rows - tap_index + frames] * grad_mixed_f,
                axis=0,
            )
            for tap_index in range(tap_count)
        ]
    )
    all_devices = data_devices * seq_devices
    taps_flat = taps_terms.reshape(all_devices, -1)
    lane = 128
    proj_terms = jnp.einsum("tc,tj->cj", signal, grad_rows, preferred_element_type=jnp.float32)
    row_block = proj_terms.shape[0] // all_devices
    proj_flat = proj_terms.reshape(all_devices, row_block * proj_terms.shape[1] // lane, lane)
    taps_row = jnp.pad(taps_flat, ((0, 0), (0, lane - taps_flat.shape[1])))[:, None, :]
    proj_parts = jnp.sum(
        lax.all_to_all(
            jnp.concatenate([proj_flat, taps_row], axis=1),
            ("dp", "seq"),
            split_axis=0,
            concat_axis=0,
            tiled=True,
        ),
        axis=0,
    )
    taps_share = proj_parts[-1, : taps_flat.shape[1]]
    taps_whole = lax.all_to_all(
        jnp.broadcast_to(taps_share[None], taps_flat.shape),
        ("dp", "seq"),
        split_axis=0,
        concat_axis=0,
        tiled=True,
    )
    grad_taps = taps_whole.reshape(taps_terms.shape) * grad_scale
    grad_proj = proj_parts[:-1].reshape(row_block, proj_terms.shape[1]) * grad_scale
    grad_in = jnp.einsum(
        "tj,dj->td", grad_rows, proj_weight, preferred_element_type=jnp.float32
    ).astype(jnp.bfloat16)
    return (layer_out[None], grad_in[None], grad_proj, grad_taps, grad_filters)


def solution(mesh):
    placed = (P("dp", "seq", None), P(), P(), P("seq", None, None), P("dp", "seq", None))
    return jax.shard_map(
        shards,
        mesh=mesh,
        in_specs=placed,
        out_specs=(
            P("dp", "seq", None),
            P("dp", "seq", None),
            P(("dp", "seq"), None),
            P(),
            P("seq", None, "dp"),
        ),
        check_vma=False,
    )
```

```python
import math

import jax
import jax.numpy as jnp
from jax import lax
from jax.sharding import PartitionSpec as P

PRECISE = lax.Precision.HIGH
FULL_TURN = 2.0 * math.pi


def passed_along(value, axis, by):
    size = lax.axis_size(axis)
    pairs = [(i, i + by) for i in range(size) if 0 <= i + by < size]
    return lax.ppermute(value, axis, pairs)


def angle_table(row_count, col_count, period):
    products = (
        jnp.arange(row_count, dtype=jnp.int32)[:, None]
        * jnp.arange(col_count, dtype=jnp.int32)[None, :]
        % period
    )
    angles = products.astype(jnp.float32) * (FULL_TURN / period)
    return (jnp.cos(angles), jnp.sin(angles))


def rotate_stacked(stacked, cosine_table, sine_table, direction):
    return jnp.stack(
        [
            stacked[0] * cosine_table - direction * stacked[1] * sine_table,
            stacked[1] * cosine_table + direction * stacked[0] * sine_table,
        ]
    )


def dft_pair(cosine_table, sine_table, stacked, table_part, data_part, result_side, direction):
    block_table = jnp.stack(
        [
            jnp.stack([cosine_table, -direction * sine_table]),
            jnp.stack([direction * sine_table, cosine_table]),
        ]
    )
    return jnp.einsum(
        "yz" + table_part + ",z" + data_part + "->y" + result_side,
        block_table,
        stacked,
        precision=PRECISE,
    )


def spectral_product(left_side, right_side):
    return jnp.stack(
        [
            left_side[0] * right_side[0] - left_side[1] * right_side[1],
            left_side[0] * right_side[1] + left_side[1] * right_side[0],
        ]
    )


def adjoint_product(left_side, right_side):
    return jnp.stack(
        [
            left_side[0] * right_side[0] + left_side[1] * right_side[1],
            left_side[0] * right_side[1] - left_side[1] * right_side[0],
        ]
    )


def local_forward(stacked):
    local_freqs, frames, channels = (stacked.shape[1], stacked.shape[2], stacked.shape[3])
    inner_len = frames
    outer_len = frames // inner_len
    data = stacked.reshape(2, local_freqs, outer_len, inner_len, channels)
    cosine_table, sine_table = angle_table(outer_len, outer_len, outer_len)
    data = dft_pair(cosine_table, sine_table, data, "ga", "kabw", "kgbw", -1.0)
    cosine_table, sine_table = angle_table(outer_len, inner_len, frames)
    data = rotate_stacked(data, cosine_table[None, :, :, None], sine_table[None, :, :, None], -1.0)
    cosine_table, sine_table = angle_table(inner_len, inner_len, inner_len)
    data = dft_pair(cosine_table, sine_table, data, "fb", "kgbw", "kgfw", -1.0)
    return data.reshape(2, local_freqs, frames, channels)


def local_inverse(stacked):
    local_freqs, frames, channels = (stacked.shape[1], stacked.shape[2], stacked.shape[3])
    inner_len = frames
    outer_len = frames // inner_len
    data = stacked.reshape(2, local_freqs, outer_len, inner_len, channels)
    cosine_table, sine_table = angle_table(inner_len, inner_len, inner_len)
    data = dft_pair(cosine_table, sine_table, data, "bf", "kgfw", "kgbw", 1.0)
    cosine_table, sine_table = angle_table(outer_len, inner_len, frames)
    data = rotate_stacked(data, cosine_table[None, :, :, None], sine_table[None, :, :, None], 1.0)
    cosine_table, sine_table = angle_table(outer_len, outer_len, outer_len)
    data = dft_pair(cosine_table, sine_table, data, "ag", "kgbw", "kabw", 1.0)
    return data.reshape(2, local_freqs, frames, channels) / frames


def forward_transform(field):
    seq_devices = lax.axis_size("seq")
    frames, channels = field.shape
    block_rows = frames // seq_devices
    freq_rows = 2 * seq_devices
    fft_length = freq_rows * frames
    received = lax.all_to_all(
        field.reshape(seq_devices, block_rows, channels),
        "seq",
        split_axis=0,
        concat_axis=0,
        tiled=True,
    )
    values = received.astype(jnp.float32)
    cosine_table, sine_table = angle_table(seq_devices, seq_devices, freq_rows)
    alternating = jnp.where(jnp.arange(seq_devices) % 2 == 0, 1.0, -1.0).astype(jnp.float32)
    part_table = jnp.stack([cosine_table, (-sine_table).at[0].set(alternating)])
    section = jnp.einsum("ykq,qrw->ykrw", part_table, values, precision=PRECISE)
    frame_ids = lax.axis_index("seq") * block_rows + jnp.arange(block_rows, dtype=jnp.int32)
    products = (
        jnp.arange(seq_devices, dtype=jnp.int32)[:, None] * frame_ids[None, :] % fft_length
    )
    angles = products.astype(jnp.float32) * (FULL_TURN / fft_length)
    stacked = rotate_stacked(
        section, jnp.cos(angles)[:, :, None], jnp.sin(angles)[:, :, None], -1.0
    ).astype(jnp.bfloat16)
    regrouped = lax.all_to_all(stacked, "seq", split_axis=1, concat_axis=2, tiled=True)
    data = regrouped[:, 0].astype(jnp.float32)
    first_device = lax.axis_index("seq") == 0
    products = seq_devices * jnp.arange(frames, dtype=jnp.int32) % fft_length
    angles = (products.astype(jnp.float32) * (FULL_TURN / fft_length))[:, None]
    zeros = jnp.zeros_like(data[0])
    row_low = jnp.where(first_device, jnp.stack([data[0], zeros]), data)
    row_high = jnp.where(
        first_device,
        jnp.stack([jnp.cos(angles) * data[1], -jnp.sin(angles) * data[1]]),
        jnp.zeros_like(data),
    )
    return local_forward(jnp.stack([row_low, row_high], axis=1))


def inverse_transform(spectra, keep_wide):
    seq_devices = lax.axis_size("seq")
    local_freqs, frames, channels = (spectra.shape[1], spectra.shape[2], spectra.shape[3])
    block_rows = frames // seq_devices
    freq_rows = 2 * seq_devices
    fft_length = freq_rows * frames
    stacked = local_inverse(spectra)
    device = lax.axis_index("seq")
    freq_ids = jnp.stack([device, jnp.int32(seq_devices)]).astype(jnp.int32)
    products = freq_ids[:, None] * jnp.arange(frames, dtype=jnp.int32)[None, :] % fft_length
    angles = products.astype(jnp.float32) * (FULL_TURN / fft_length)
    stacked = rotate_stacked(stacked, jnp.cos(angles)[:, :, None], jnp.sin(angles)[:, :, None], 1.0)
    back = stacked.astype(jnp.bfloat16)
    packed = jnp.where(device == 0, jnp.stack([back[0, 0], back[0, 1]]), back[:, 0])
    regrouped = lax.all_to_all(
        packed[:, None], "seq", split_axis=2, concat_axis=1, tiled=True
    ).astype(jnp.float32)
    cosine_table, sine_table = angle_table(seq_devices, seq_devices, freq_rows)
    alternating = jnp.where(jnp.arange(seq_devices) % 2 == 0, 1.0, -1.0).astype(jnp.float32)
    real_table = (2.0 * cosine_table).at[:, 0].set(1.0)
    imag_table = (-2.0 * sine_table).at[:, 0].set(alternating)
    part_table = jnp.stack([real_table, imag_table]) / freq_rows
    values = jnp.einsum("zqk,zkrw->qrw", part_table, regrouped, precision=PRECISE)
    returned = lax.all_to_all(
        values.astype(jnp.bfloat16), "seq", split_axis=0, concat_axis=1, tiled=True
    )
    return returned.reshape(frames, channels)


def shards(frames_in, proj_weight, conv_taps, long_filters, out_grad):
    signal = frames_in[0]
    frames, channels = signal.shape
    seq_devices = lax.axis_size("seq")
    data_devices = lax.axis_size("dp")
    grad_scale = 1.0 / math.sqrt(data_devices * seq_devices * frames)
    margin_rows = conv_taps.shape[0] - 1
    tap_count = conv_taps.shape[0]
    projected = jnp.dot(signal, proj_weight, preferred_element_type=jnp.float32).astype(
        jnp.bfloat16
    )
    before = passed_along(projected[frames - margin_rows :], "seq", 1)
    extended = jnp.concatenate([before, projected], axis=0).astype(jnp.float32)
    mixed = sum(
        (
            conv_taps[tap_index][None, :]
            * extended[margin_rows - tap_index : margin_rows - tap_index + frames]
            for tap_index in range(tap_count)
        )
    ).astype(jnp.bfloat16)
    value = mixed[:, :channels]
    gate_one = mixed[:, channels : 2 * channels].astype(jnp.float32)
    gate_two = mixed[:, 2 * channels :].astype(jnp.float32)
    upstream = out_grad[0].astype(jnp.float32)
    grad_two = (upstream * gate_two).astype(jnp.bfloat16)
    opening = forward_transform(
        jnp.concatenate([long_filters.reshape(frames, 2 * channels), value, grad_two], axis=1)
    )
    filter_one = opening[..., :channels]
    filter_two = opening[..., channels : 2 * channels]
    value_spectra = opening[..., 2 * channels : 3 * channels]
    two_spectra = opening[..., 3 * channels :]
    middle_rows = inverse_transform(
        jnp.concatenate(
            [
                spectral_product(filter_one, value_spectra),
                adjoint_product(filter_two, two_spectra),
            ],
            axis=3,
        ),
        False,
    )
    conv_one = middle_rows[:, :channels]
    grad_first = middle_rows[:, channels:]
    first = (gate_one * conv_one.astype(jnp.float32)).astype(jnp.bfloat16)
    grad_one = (grad_first.astype(jnp.float32) * gate_one).astype(jnp.bfloat16)
    second = forward_transform(jnp.concatenate([first, grad_one], axis=1))
    first_spectra = second[..., :channels]
    one_spectra = second[..., channels:]
    closing = inverse_transform(
        jnp.concatenate(
            [
                spectral_product(filter_two, first_spectra),
                adjoint_product(filter_one, one_spectra),
                adjoint_product(value_spectra, one_spectra),
                adjoint_product(first_spectra, two_spectra),
            ],
            axis=3,
        ),
        False,
    )
    conv_two = closing[:, :channels]
    grad_value = closing[:, channels : 2 * channels]
    tap_rows = closing[:, 2 * channels :]
    block = channels // data_devices
    tap_blocks = tap_rows.reshape(frames, 2, data_devices, block).transpose(2, 1, 0, 3)
    tap_parts = lax.all_to_all(tap_blocks, "dp", split_axis=0, concat_axis=0, tiled=True)
    grad_filters = (
        jnp.sum(tap_parts.astype(jnp.float32), axis=0).transpose(1, 0, 2) * grad_scale
    )
    middle = (grad_first.astype(jnp.float32) * conv_one.astype(jnp.float32)).astype(jnp.bfloat16)
    layer_out = (gate_two * conv_two.astype(jnp.float32)).astype(jnp.bfloat16)
    grad_mixed = jnp.concatenate(
        [
            grad_value.astype(jnp.float32),
            middle.astype(jnp.float32),
            upstream * conv_two.astype(jnp.float32),
        ],
        axis=1,
    ).astype(jnp.bfloat16)
    after_rows = passed_along(grad_mixed[:margin_rows], "seq", -1)
    grad_mixed_f = grad_mixed.astype(jnp.float32)
    grad_pad = jnp.concatenate([grad_mixed, after_rows], axis=0).astype(jnp.float32)
    grad_rows = sum(
        (
            conv_taps[tap_index][None, :] * grad_pad[tap_index : tap_index + frames]
            for tap_index in range(tap_count)
        )
    ).astype(jnp.bfloat16)
    taps_terms = jnp.stack(
        [
            jnp.sum(
                extended[margin_rows - tap_index : margin_rows - tap_index + frames] * grad_mixed_f,
                axis=0,
            )
            for tap_index in range(tap_count)
        ]
    )
    all_devices = data_devices * seq_devices
    taps_flat = taps_terms.reshape(all_devices, -1)
    lane = 128
    proj_terms = jnp.einsum("tc,tj->cj", signal, grad_rows, preferred_element_type=jnp.float32)
    row_block = proj_terms.shape[0] // all_devices
    proj_flat = proj_terms.reshape(all_devices, row_block * proj_terms.shape[1] // lane, lane)
    taps_row = jnp.pad(taps_flat, ((0, 0), (0, lane - taps_flat.shape[1])))[:, None, :]
    proj_parts = jnp.sum(
        lax.all_to_all(
            jnp.concatenate([proj_flat, taps_row], axis=1),
            ("dp", "seq"),
            split_axis=0,
            concat_axis=0,
            tiled=True,
        ),
        axis=0,
    )
    taps_share = proj_parts[-1, : taps_flat.shape[1]]
    taps_whole = lax.all_to_all(
        jnp.broadcast_to(taps_share[None], taps_flat.shape),
        ("dp", "seq"),
        split_axis=0,
        concat_axis=0,
        tiled=True,
    )
    grad_taps = taps_whole.reshape(taps_terms.shape) * grad_scale
    grad_proj = proj_parts[:-1].reshape(row_block, proj_terms.shape[1]) * grad_scale
    grad_in = jnp.einsum(
        "tj,dj->td", grad_rows, proj_weight, preferred_element_type=jnp.float32
    ).astype(jnp.bfloat16)
    return (layer_out[None], grad_in[None], grad_proj, grad_taps, grad_filters)


def solution(mesh):
    placed = (P("dp", "seq", None), P(), P(), P("seq", None, None), P("dp", "seq", None))
    return jax.shard_map(
        shards,
        mesh=mesh,
        in_specs=placed,
        out_specs=(
            P("dp", "seq", None),
            P("dp", "seq", None),
            P(("dp", "seq"), None),
            P(),
            P("seq", None, "dp"),
        ),
        check_vma=False,
    )
```

```python
import math

import jax
import jax.numpy as jnp
from jax import lax
from jax.sharding import PartitionSpec as P

PRECISE = lax.Precision.HIGH
FULL_TURN = 2.0 * math.pi


def passed_along(value, axis, by):
    size = lax.axis_size(axis)
    pairs = [(i, i + by) for i in range(size) if 0 <= i + by < size]
    return lax.ppermute(value, axis, pairs)


def angle_table(row_count, col_count, period):
    products = (
        jnp.arange(row_count, dtype=jnp.int32)[:, None]
        * jnp.arange(col_count, dtype=jnp.int32)[None, :]
        % period
    )
    angles = products.astype(jnp.float32) * (FULL_TURN / period)
    return (jnp.cos(angles), jnp.sin(angles))


def rotate_stacked(stacked, cosine_table, sine_table, direction):
    return jnp.stack(
        [
            stacked[0] * cosine_table - direction * stacked[1] * sine_table,
            stacked[1] * cosine_table + direction * stacked[0] * sine_table,
        ]
    )


def dft_pair(cosine_table, sine_table, stacked, table_part, data_part, result_side, direction):
    block_table = jnp.stack(
        [
            jnp.stack([cosine_table, -direction * sine_table]),
            jnp.stack([direction * sine_table, cosine_table]),
        ]
    )
    return jnp.einsum(
        "yz" + table_part + ",z" + data_part + "->y" + result_side,
        block_table,
        stacked,
        precision=PRECISE,
    )


def spectral_product(left_side, right_side):
    return jnp.stack(
        [
            left_side[0] * right_side[0] - left_side[1] * right_side[1],
            left_side[0] * right_side[1] + left_side[1] * right_side[0],
        ]
    )


def adjoint_product(left_side, right_side):
    return jnp.stack(
        [
            left_side[0] * right_side[0] + left_side[1] * right_side[1],
            left_side[0] * right_side[1] - left_side[1] * right_side[0],
        ]
    )


def local_forward(stacked):
    local_freqs, frames, channels = (stacked.shape[1], stacked.shape[2], stacked.shape[3])
    inner_len = math.gcd(frames, 128)
    outer_len = frames // inner_len
    data = stacked.reshape(2, local_freqs, outer_len, inner_len, channels)
    cosine_table, sine_table = angle_table(outer_len, outer_len, outer_len)
    data = dft_pair(cosine_table, sine_table, data, "ga", "kabw", "kgbw", -1.0)
    cosine_table, sine_table = angle_table(outer_len, inner_len, frames)
    data = rotate_stacked(data, cosine_table[None, :, :, None], sine_table[None, :, :, None], -1.0)
    cosine_table, sine_table = angle_table(inner_len, inner_len, inner_len)
    data = dft_pair(cosine_table, sine_table, data, "fb", "kgbw", "kgfw", -1.0)
    return data.reshape(2, local_freqs, frames, channels)


def local_inverse(stacked):
    local_freqs, frames, channels = (stacked.shape[1], stacked.shape[2], stacked.shape[3])
    inner_len = math.gcd(frames, 128)
    outer_len = frames // inner_len
    data = stacked.reshape(2, local_freqs, outer_len, inner_len, channels)
    cosine_table, sine_table = angle_table(inner_len, inner_len, inner_len)
    data = dft_pair(cosine_table, sine_table, data, "bf", "kgfw", "kgbw", 1.0)
    cosine_table, sine_table = angle_table(outer_len, inner_len, frames)
    data = rotate_stacked(data, cosine_table[None, :, :, None], sine_table[None, :, :, None], 1.0)
    cosine_table, sine_table = angle_table(outer_len, outer_len, outer_len)
    data = dft_pair(cosine_table, sine_table, data, "ag", "kgbw", "kabw", 1.0)
    return data.reshape(2, local_freqs, frames, channels) / frames


def forward_gather(field):
    seq_devices = lax.axis_size("seq")
    frames, channels = field.shape
    block_rows = frames // seq_devices
    return lax.all_to_all(
        field.reshape(seq_devices, block_rows, channels),
        "seq",
        split_axis=0,
        concat_axis=0,
        tiled=True,
    )


def forward_transform(field):
    return forward_core(forward_gather(field))


def forward_core(received):
    seq_devices = lax.axis_size("seq")
    block_rows = received.shape[1]
    frames = seq_devices * block_rows
    freq_rows = 2 * seq_devices
    fft_length = freq_rows * frames
    values = received.astype(jnp.float32)
    cosine_table, sine_table = angle_table(seq_devices, seq_devices, freq_rows)
    alternating = jnp.where(jnp.arange(seq_devices) % 2 == 0, 1.0, -1.0).astype(jnp.float32)
    part_table = jnp.stack([cosine_table, (-sine_table).at[0].set(alternating)])
    section = jnp.einsum("ykq,qrw->ykrw", part_table, values, precision=PRECISE)
    frame_ids = lax.axis_index("seq") * block_rows + jnp.arange(block_rows, dtype=jnp.int32)
    products = (
        jnp.arange(seq_devices, dtype=jnp.int32)[:, None] * frame_ids[None, :] % fft_length
    )
    angles = products.astype(jnp.float32) * (FULL_TURN / fft_length)
    stacked = rotate_stacked(
        section, jnp.cos(angles)[:, :, None], jnp.sin(angles)[:, :, None], -1.0
    ).astype(jnp.bfloat16)
    regrouped = lax.all_to_all(stacked, "seq", split_axis=1, concat_axis=2, tiled=True)
    data = regrouped[:, 0].astype(jnp.float32)
    first_device = lax.axis_index("seq") == 0
    products = seq_devices * jnp.arange(frames, dtype=jnp.int32) % fft_length
    angles = (products.astype(jnp.float32) * (FULL_TURN / fft_length))[:, None]
    zeros = jnp.zeros_like(data[0])
    row_low = jnp.where(first_device, jnp.stack([data[0], zeros]), data)
    row_high = jnp.where(
        first_device,
        jnp.stack([jnp.cos(angles) * data[1], -jnp.sin(angles) * data[1]]),
        jnp.zeros_like(data),
    )
    return local_forward(jnp.stack([row_low, row_high], axis=1))


def inverse_core(spectra):
    seq_devices = lax.axis_size("seq")
    local_freqs, frames, channels = (spectra.shape[1], spectra.shape[2], spectra.shape[3])
    block_rows = frames // seq_devices
    freq_rows = 2 * seq_devices
    fft_length = freq_rows * frames
    stacked = local_inverse(spectra)
    device = lax.axis_index("seq")
    freq_ids = jnp.stack([device, jnp.int32(seq_devices)]).astype(jnp.int32)
    products = freq_ids[:, None] * jnp.arange(frames, dtype=jnp.int32)[None, :] % fft_length
    angles = products.astype(jnp.float32) * (FULL_TURN / fft_length)
    stacked = rotate_stacked(stacked, jnp.cos(angles)[:, :, None], jnp.sin(angles)[:, :, None], 1.0)
    back = stacked.astype(jnp.bfloat16)
    packed = jnp.where(device == 0, jnp.stack([back[0, 0], back[0, 1]]), back[:, 0])
    regrouped = lax.all_to_all(
        packed[:, None], "seq", split_axis=2, concat_axis=1, tiled=True
    ).astype(jnp.float32)
    cosine_table, sine_table = angle_table(seq_devices, seq_devices, freq_rows)
    alternating = jnp.where(jnp.arange(seq_devices) % 2 == 0, 1.0, -1.0).astype(jnp.float32)
    real_table = (2.0 * cosine_table).at[:, 0].set(1.0)
    imag_table = (-2.0 * sine_table).at[:, 0].set(alternating)
    part_table = jnp.stack([real_table, imag_table]) / freq_rows
    return jnp.einsum("zqk,zkrw->qrw", part_table, regrouped, precision=PRECISE)


def inverse_scatter(values):
    seq_devices, block_rows, channels = values.shape
    returned = lax.all_to_all(
        values.astype(jnp.bfloat16), "seq", split_axis=0, concat_axis=1, tiled=True
    )
    return returned.reshape(seq_devices * block_rows, channels)


def inverse_transform(spectra, keep_wide):
    return inverse_scatter(inverse_core(spectra))


def shards(frames_in, proj_weight, conv_taps, long_filters, out_grad):
    signal = frames_in[0]
    frames, channels = signal.shape
    seq_devices = lax.axis_size("seq")
    data_devices = lax.axis_size("dp")
    grad_scale = 1.0 / math.sqrt(data_devices * seq_devices * frames)
    margin_rows = conv_taps.shape[0] - 1
    tap_count = conv_taps.shape[0]
    projected = jnp.dot(signal, proj_weight, preferred_element_type=jnp.float32).astype(
        jnp.bfloat16
    )
    before = passed_along(projected[frames - margin_rows :], "seq", 1)
    extended = jnp.concatenate([before, projected], axis=0).astype(jnp.float32)
    mixed = sum(
        (
            conv_taps[tap_index][None, :]
            * extended[margin_rows - tap_index : margin_rows - tap_index + frames]
            for tap_index in range(tap_count)
        )
    ).astype(jnp.bfloat16)
    value = mixed[:, :channels]
    gate_one = mixed[:, channels : 2 * channels].astype(jnp.float32)
    gate_two = mixed[:, 2 * channels :].astype(jnp.float32)
    upstream = out_grad[0].astype(jnp.float32)
    grad_two = (upstream * gate_two).astype(jnp.bfloat16)
    opening_rows = forward_gather(
        jnp.concatenate(
            [
                long_filters.reshape(frames, 2 * channels),
                value,
                grad_two,
                mixed[:, channels : 2 * channels],
            ],
            axis=1,
        )
    )
    opening = forward_core(opening_rows[..., : 4 * channels])
    gate_one_blocks = opening_rows[..., 4 * channels :].astype(jnp.float32)
    filter_one = opening[..., :channels]
    filter_two = opening[..., channels : 2 * channels]
    value_spectra = opening[..., 2 * channels : 3 * channels]
    two_spectra = opening[..., 3 * channels :]
    middle_rows = inverse_core(
        jnp.concatenate(
            [
                spectral_product(filter_one, value_spectra),
                adjoint_product(filter_two, two_spectra),
            ],
            axis=3,
        )
    ).astype(jnp.bfloat16)
    conv_one_blocks = middle_rows[..., :channels].astype(jnp.float32)
    grad_first_blocks = middle_rows[..., channels:].astype(jnp.float32)
    first = (gate_one_blocks * conv_one_blocks).astype(jnp.bfloat16)
    grad_one = (grad_first_blocks * gate_one_blocks).astype(jnp.bfloat16)
    middle = inverse_scatter((grad_first_blocks * conv_one_blocks).astype(jnp.bfloat16))
    second = forward_core(jnp.concatenate([first, grad_one], axis=2))
    first_spectra = second[..., :channels]
    one_spectra = second[..., channels:]
    closing = inverse_transform(
        jnp.concatenate(
            [
                spectral_product(filter_two, first_spectra),
                adjoint_product(filter_one, one_spectra),
                adjoint_product(value_spectra, one_spectra),
                adjoint_product(first_spectra, two_spectra),
            ],
            axis=3,
        ),
        False,
    )
    conv_two = closing[:, :channels]
    grad_value = closing[:, channels : 2 * channels]
    tap_rows = closing[:, 2 * channels :]
    block = channels // data_devices
    tap_blocks = tap_rows.reshape(frames, 2, data_devices, block).transpose(2, 1, 0, 3)
    tap_parts = lax.all_to_all(tap_blocks, "dp", split_axis=0, concat_axis=0, tiled=True)
    grad_filters = (
        jnp.sum(tap_parts.astype(jnp.float32), axis=0).transpose(1, 0, 2) * grad_scale
    )
    layer_out = (gate_two * conv_two.astype(jnp.float32)).astype(jnp.bfloat16)
    grad_mixed = jnp.concatenate(
        [
            grad_value.astype(jnp.float32),
            middle.astype(jnp.float32),
            upstream * conv_two.astype(jnp.float32),
        ],
        axis=1,
    ).astype(jnp.bfloat16)
    after_rows = passed_along(grad_mixed[:margin_rows], "seq", -1)
    grad_mixed_f = grad_mixed.astype(jnp.float32)
    grad_pad = jnp.concatenate([grad_mixed, after_rows], axis=0).astype(jnp.float32)
    grad_rows = sum(
        (
            conv_taps[tap_index][None, :] * grad_pad[tap_index : tap_index + frames]
            for tap_index in range(tap_count)
        )
    ).astype(jnp.bfloat16)
    taps_terms = jnp.stack(
        [
            jnp.sum(
                extended[margin_rows - tap_index : margin_rows - tap_index + frames] * grad_mixed_f,
                axis=0,
            )
            for tap_index in range(tap_count)
        ]
    )
    all_devices = data_devices * seq_devices
    taps_flat = taps_terms.reshape(all_devices, -1)
    lane = 128
    proj_terms = jnp.einsum("tc,tj->cj", signal, grad_rows, preferred_element_type=jnp.float32)
    row_block = proj_terms.shape[0] // all_devices
    proj_flat = proj_terms.reshape(all_devices, row_block * proj_terms.shape[1] // lane, lane)
    taps_row = jnp.pad(taps_flat, ((0, 0), (0, lane - taps_flat.shape[1])))[:, None, :]
    proj_parts = jnp.sum(
        lax.all_to_all(
            jnp.concatenate([proj_flat, taps_row], axis=1),
            ("dp", "seq"),
            split_axis=0,
            concat_axis=0,
            tiled=True,
        ),
        axis=0,
    )
    taps_share = proj_parts[-1, : taps_flat.shape[1]]
    taps_whole = lax.all_to_all(
        jnp.broadcast_to(taps_share[None], taps_flat.shape),
        ("dp", "seq"),
        split_axis=0,
        concat_axis=0,
        tiled=True,
    )
    grad_taps = taps_whole.reshape(taps_terms.shape) * grad_scale
    grad_proj = proj_parts[:-1].reshape(row_block, proj_terms.shape[1]) * grad_scale
    grad_in = jnp.einsum(
        "tj,dj->td", grad_rows, proj_weight, preferred_element_type=jnp.float32
    ).astype(jnp.bfloat16)
    return (layer_out[None], grad_in[None], grad_proj, grad_taps, grad_filters)


def solution(mesh):
    placed = (P("dp", "seq", None), P(), P(), P("seq", None, None), P("dp", "seq", None))
    return jax.shard_map(
        shards,
        mesh=mesh,
        in_specs=placed,
        out_specs=(
            P("dp", "seq", None),
            P("dp", "seq", None),
            P(("dp", "seq"), None),
            P(),
            P("seq", None, "dp"),
        ),
        check_vma=False,
    )
```

```python
import math

import jax
import jax.numpy as jnp
from jax import lax
from jax.sharding import PartitionSpec as P

PRECISE = lax.Precision.HIGH
FULL_TURN = 2.0 * math.pi


def passed_along(value, axis, by):
    size = lax.axis_size(axis)
    pairs = [(i, i + by) for i in range(size) if 0 <= i + by < size]
    return lax.ppermute(value, axis, pairs)


def angle_table(row_count, col_count, period):
    products = (
        jnp.arange(row_count, dtype=jnp.int32)[:, None]
        * jnp.arange(col_count, dtype=jnp.int32)[None, :]
        % period
    )
    angles = products.astype(jnp.float32) * (FULL_TURN / period)
    return (jnp.cos(angles), jnp.sin(angles))


def rotate_stacked(stacked, cosine_table, sine_table, direction):
    return jnp.stack(
        [
            stacked[0] * cosine_table - direction * stacked[1] * sine_table,
            stacked[1] * cosine_table + direction * stacked[0] * sine_table,
        ]
    )


def dft_pair(cosine_table, sine_table, stacked, table_part, data_part, result_side, direction):
    block_table = jnp.stack(
        [
            jnp.stack([cosine_table, -direction * sine_table]),
            jnp.stack([direction * sine_table, cosine_table]),
        ]
    )
    return jnp.einsum(
        "yz" + table_part + ",z" + data_part + "->y" + result_side,
        block_table,
        stacked,
        precision=PRECISE,
    )


def spectral_product(left_side, right_side):
    return jnp.stack(
        [
            left_side[0] * right_side[0] - left_side[1] * right_side[1],
            left_side[0] * right_side[1] + left_side[1] * right_side[0],
        ]
    )


def adjoint_product(left_side, right_side):
    return jnp.stack(
        [
            left_side[0] * right_side[0] + left_side[1] * right_side[1],
            left_side[0] * right_side[1] - left_side[1] * right_side[0],
        ]
    )


def local_forward(stacked):
    local_freqs, frames, channels = (stacked.shape[1], stacked.shape[2], stacked.shape[3])
    inner_len = math.gcd(frames, 128)
    outer_len = frames // inner_len
    data = stacked.reshape(2, local_freqs, outer_len, inner_len, channels)
    cosine_table, sine_table = angle_table(outer_len, outer_len, outer_len)
    data = dft_pair(cosine_table, sine_table, data, "ga", "kabw", "kgbw", -1.0)
    cosine_table, sine_table = angle_table(outer_len, inner_len, frames)
    data = rotate_stacked(data, cosine_table[None, :, :, None], sine_table[None, :, :, None], -1.0)
    cosine_table, sine_table = angle_table(inner_len, inner_len, inner_len)
    data = dft_pair(cosine_table, sine_table, data, "fb", "kgbw", "kgfw", -1.0)
    return data.reshape(2, local_freqs, frames, channels)


def local_inverse(stacked):
    local_freqs, frames, channels = (stacked.shape[1], stacked.shape[2], stacked.shape[3])
    inner_len = math.gcd(frames, 128)
    outer_len = frames // inner_len
    data = stacked.reshape(2, local_freqs, outer_len, inner_len, channels)
    cosine_table, sine_table = angle_table(inner_len, inner_len, inner_len)
    data = dft_pair(cosine_table, sine_table, data, "bf", "kgfw", "kgbw", 1.0)
    cosine_table, sine_table = angle_table(outer_len, inner_len, frames)
    data = rotate_stacked(data, cosine_table[None, :, :, None], sine_table[None, :, :, None], 1.0)
    cosine_table, sine_table = angle_table(outer_len, outer_len, outer_len)
    data = dft_pair(cosine_table, sine_table, data, "ag", "kgbw", "kabw", 1.0)
    return data.reshape(2, local_freqs, frames, channels) / frames


def forward_gather(field):
    seq_devices = lax.axis_size("seq")
    frames, channels = field.shape
    block_rows = frames // seq_devices
    return lax.all_to_all(
        field.reshape(seq_devices, block_rows, channels),
        "seq",
        split_axis=0,
        concat_axis=0,
        tiled=True,
    )


def forward_transform(field):
    return forward_core(forward_gather(field))


def forward_core(received):
    seq_devices = lax.axis_size("seq")
    block_rows = received.shape[1]
    frames = seq_devices * block_rows
    freq_rows = 2 * seq_devices
    fft_length = freq_rows * frames
    values = received.astype(jnp.float32)
    cosine_table, sine_table = angle_table(seq_devices, seq_devices, freq_rows)
    alternating = jnp.where(jnp.arange(seq_devices) % 2 == 0, 1.0, -1.0).astype(jnp.float32)
    part_table = jnp.stack([cosine_table, (-sine_table).at[0].set(alternating)])
    section = jnp.einsum("ykq,qrw->ykrw", part_table, values, precision=PRECISE)
    frame_ids = lax.axis_index("seq") * block_rows + jnp.arange(block_rows, dtype=jnp.int32)
    products = (
        jnp.arange(seq_devices, dtype=jnp.int32)[:, None] * frame_ids[None, :] % fft_length
    )
    angles = products.astype(jnp.float32) * (FULL_TURN / fft_length)
    stacked = rotate_stacked(
        section, jnp.cos(angles)[:, :, None], jnp.sin(angles)[:, :, None], -1.0
    ).astype(jnp.bfloat16)
    regrouped = lax.all_to_all(stacked, "seq", split_axis=1, concat_axis=2, tiled=True)
    data = regrouped[:, 0].astype(jnp.float32)
    first_device = lax.axis_index("seq") == 0
    products = seq_devices * jnp.arange(frames, dtype=jnp.int32) % fft_length
    angles = (products.astype(jnp.float32) * (FULL_TURN / fft_length))[:, None]
    zeros = jnp.zeros_like(data[0])
    row_low = jnp.where(first_device, jnp.stack([data[0], zeros]), data)
    row_high = jnp.where(
        first_device,
        jnp.stack([jnp.cos(angles) * data[1], -jnp.sin(angles) * data[1]]),
        jnp.zeros_like(data),
    )
    return local_forward(jnp.stack([row_low, row_high], axis=1))


def inverse_core(spectra):
    seq_devices = lax.axis_size("seq")
    local_freqs, frames, channels = (spectra.shape[1], spectra.shape[2], spectra.shape[3])
    block_rows = frames // seq_devices
    freq_rows = 2 * seq_devices
    fft_length = freq_rows * frames
    stacked = local_inverse(spectra)
    device = lax.axis_index("seq")
    freq_ids = jnp.stack([device, jnp.int32(seq_devices)]).astype(jnp.int32)
    products = freq_ids[:, None] * jnp.arange(frames, dtype=jnp.int32)[None, :] % fft_length
    angles = products.astype(jnp.float32) * (FULL_TURN / fft_length)
    stacked = rotate_stacked(stacked, jnp.cos(angles)[:, :, None], jnp.sin(angles)[:, :, None], 1.0)
    back = stacked.astype(jnp.bfloat16)
    packed = jnp.where(device == 0, jnp.stack([back[0, 0], back[0, 1]]), back[:, 0])
    regrouped = lax.all_to_all(
        packed[:, None], "seq", split_axis=2, concat_axis=1, tiled=True
    ).astype(jnp.float32)
    cosine_table, sine_table = angle_table(seq_devices, seq_devices, freq_rows)
    alternating = jnp.where(jnp.arange(seq_devices) % 2 == 0, 1.0, -1.0).astype(jnp.float32)
    real_table = (2.0 * cosine_table).at[:, 0].set(1.0)
    imag_table = (-2.0 * sine_table).at[:, 0].set(alternating)
    part_table = jnp.stack([real_table, imag_table]) / freq_rows
    return jnp.einsum("zqk,zkrw->qrw", part_table, regrouped, precision=PRECISE)


def inverse_scatter(values):
    seq_devices, block_rows, channels = values.shape
    returned = lax.all_to_all(
        values.astype(jnp.bfloat16), "seq", split_axis=0, concat_axis=1, tiled=True
    )
    return returned.reshape(seq_devices * block_rows, channels)


def inverse_transform(spectra, keep_wide):
    return inverse_scatter(inverse_core(spectra))


def shards(frames_in, proj_weight, conv_taps, long_filters, out_grad):
    signal = frames_in[0]
    frames, channels = signal.shape
    seq_devices = lax.axis_size("seq")
    data_devices = lax.axis_size("dp")
    grad_scale = 1.0 / math.sqrt(data_devices * seq_devices * frames)
    margin_rows = conv_taps.shape[0] - 1
    tap_count = conv_taps.shape[0]
    projected = jnp.dot(signal, proj_weight, preferred_element_type=jnp.float32).astype(
        jnp.bfloat16
    )
    before = passed_along(projected[frames - margin_rows :], "seq", 1)
    extended = jnp.concatenate([before, projected], axis=0).astype(jnp.float32)
    mixed = sum(
        (
            conv_taps[tap_index][None, :]
            * extended[margin_rows - tap_index : margin_rows - tap_index + frames]
            for tap_index in range(tap_count)
        )
    ).astype(jnp.bfloat16)
    value = mixed[:, :channels]
    gate_one = mixed[:, channels : 2 * channels].astype(jnp.float32)
    gate_two = mixed[:, 2 * channels :].astype(jnp.float32)
    upstream = out_grad[0].astype(jnp.float32)
    grad_two = (upstream * gate_two).astype(jnp.bfloat16)
    opening_rows = forward_gather(
        jnp.concatenate(
            [
                long_filters.reshape(frames, 2 * channels),
                value,
                grad_two,
                mixed[:, channels : 2 * channels],
            ],
            axis=1,
        )
    )
    opening = forward_core(opening_rows[..., : 4 * channels])
    gate_one_blocks = opening_rows[..., 4 * channels :].astype(jnp.float32)
    filter_one = opening[..., :channels]
    filter_two = opening[..., channels : 2 * channels]
    value_spectra = opening[..., 2 * channels : 3 * channels]
    two_spectra = opening[..., 3 * channels :]
    middle_rows = inverse_core(
        jnp.concatenate(
            [
                spectral_product(filter_one, value_spectra),
                adjoint_product(filter_two, two_spectra),
            ],
            axis=3,
        )
    ).astype(jnp.bfloat16)
    conv_one_blocks = middle_rows[..., :channels].astype(jnp.float32)
    grad_first_blocks = middle_rows[..., channels:].astype(jnp.float32)
    first = (gate_one_blocks * conv_one_blocks).astype(jnp.bfloat16)
    grad_one = (grad_first_blocks * gate_one_blocks).astype(jnp.bfloat16)
    middle = inverse_scatter((grad_first_blocks * conv_one_blocks).astype(jnp.bfloat16))
    second = forward_core(jnp.concatenate([first, grad_one], axis=2))
    first_spectra = second[..., :channels]
    one_spectra = second[..., channels:]
    closing = inverse_core(
        jnp.concatenate(
            [
                spectral_product(filter_two, first_spectra),
                adjoint_product(filter_one, one_spectra),
                adjoint_product(value_spectra, one_spectra),
                adjoint_product(first_spectra, two_spectra),
            ],
            axis=3,
        )
    )
    closing_rows = inverse_scatter(closing[..., : 2 * channels])
    conv_two = closing_rows[:, :channels]
    grad_value = closing_rows[:, channels:]
    block = channels // data_devices
    tap_blocks = (
        closing[..., 2 * channels :]
        .astype(jnp.bfloat16)
        .reshape(seq_devices, frames // seq_devices, 2, data_devices, block)
        .transpose(3, 0, 1, 2, 4)
        .reshape(data_devices, seq_devices, frames // seq_devices, 2 * block)
    )
    tap_parts = lax.all_to_all(tap_blocks, "dp", split_axis=0, concat_axis=0, tiled=True)
    tap_sums = jnp.sum(tap_parts.astype(jnp.float32), axis=0)
    tap_rows = lax.all_to_all(tap_sums, "seq", split_axis=0, concat_axis=1, tiled=True)
    grad_filters = tap_rows.reshape(frames, 2, block) * grad_scale
    layer_out = (gate_two * conv_two.astype(jnp.float32)).astype(jnp.bfloat16)
    grad_mixed = jnp.concatenate(
        [
            grad_value.astype(jnp.float32),
            middle.astype(jnp.float32),
            upstream * conv_two.astype(jnp.float32),
        ],
        axis=1,
    ).astype(jnp.bfloat16)
    after_rows = passed_along(grad_mixed[:margin_rows], "seq", -1)
    grad_mixed_f = grad_mixed.astype(jnp.float32)
    grad_pad = jnp.concatenate([grad_mixed, after_rows], axis=0).astype(jnp.float32)
    grad_rows = sum(
        (
            conv_taps[tap_index][None, :] * grad_pad[tap_index : tap_index + frames]
            for tap_index in range(tap_count)
        )
    ).astype(jnp.bfloat16)
    taps_terms = jnp.stack(
        [
            jnp.sum(
                extended[margin_rows - tap_index : margin_rows - tap_index + frames] * grad_mixed_f,
                axis=0,
            )
            for tap_index in range(tap_count)
        ]
    )
    all_devices = data_devices * seq_devices
    taps_flat = taps_terms.reshape(all_devices, -1)
    lane = 128
    proj_terms = jnp.einsum("tc,tj->cj", signal, grad_rows, preferred_element_type=jnp.float32)
    row_block = proj_terms.shape[0] // all_devices
    proj_flat = proj_terms.reshape(all_devices, row_block * proj_terms.shape[1] // lane, lane)
    taps_row = jnp.pad(taps_flat, ((0, 0), (0, lane - taps_flat.shape[1])))[:, None, :]
    proj_parts = jnp.sum(
        lax.all_to_all(
            jnp.concatenate([proj_flat, taps_row], axis=1),
            ("dp", "seq"),
            split_axis=0,
            concat_axis=0,
            tiled=True,
        ),
        axis=0,
    )
    taps_share = proj_parts[-1, : taps_flat.shape[1]]
    taps_whole = lax.all_to_all(
        jnp.broadcast_to(taps_share[None], taps_flat.shape),
        ("dp", "seq"),
        split_axis=0,
        concat_axis=0,
        tiled=True,
    )
    grad_taps = taps_whole.reshape(taps_terms.shape) * grad_scale
    grad_proj = proj_parts[:-1].reshape(row_block, proj_terms.shape[1]) * grad_scale
    grad_in = jnp.einsum(
        "tj,dj->td", grad_rows, proj_weight, preferred_element_type=jnp.float32
    ).astype(jnp.bfloat16)
    return (layer_out[None], grad_in[None], grad_proj, grad_taps, grad_filters)


def solution(mesh):
    placed = (P("dp", "seq", None), P(), P(), P("seq", None, None), P("dp", "seq", None))
    return jax.shard_map(
        shards,
        mesh=mesh,
        in_specs=placed,
        out_specs=(
            P("dp", "seq", None),
            P("dp", "seq", None),
            P(("dp", "seq"), None),
            P(),
            P("seq", None, "dp"),
        ),
        check_vma=False,
    )
```

```python
import math

import jax
import jax.numpy as jnp
from jax import lax
from jax.sharding import PartitionSpec as P

PRECISE = lax.Precision.HIGH
FULL_TURN = 2.0 * math.pi


def passed_along(value, axis, by):
    size = lax.axis_size(axis)
    pairs = [(i, i + by) for i in range(size) if 0 <= i + by < size]
    return lax.ppermute(value, axis, pairs)


def angle_table(row_count, col_count, period):
    products = (
        jnp.arange(row_count, dtype=jnp.int32)[:, None]
        * jnp.arange(col_count, dtype=jnp.int32)[None, :]
        % period
    )
    angles = products.astype(jnp.float32) * (FULL_TURN / period)
    return (jnp.cos(angles), jnp.sin(angles))


def rotate_stacked(stacked, cosine_table, sine_table, direction):
    return jnp.stack(
        [
            stacked[0] * cosine_table - direction * stacked[1] * sine_table,
            stacked[1] * cosine_table + direction * stacked[0] * sine_table,
        ]
    )


def dft_pair(cosine_table, sine_table, stacked, table_part, data_part, result_side, direction):
    block_table = jnp.stack(
        [
            jnp.stack([cosine_table, -direction * sine_table]),
            jnp.stack([direction * sine_table, cosine_table]),
        ]
    )
    return jnp.einsum(
        "yz" + table_part + ",z" + data_part + "->y" + result_side,
        block_table,
        stacked,
        precision=PRECISE,
    )


def outer_pair(cosine_table, sine_table, stacked, table_part, data_part, result_side, direction):
    if stacked.shape[2] != 2:
        return dft_pair(
            cosine_table, sine_table, stacked, table_part, data_part, result_side, direction
        )
    return jnp.stack([stacked[:, :, 0] + stacked[:, :, 1], stacked[:, :, 0] - stacked[:, :, 1]], axis=2)


def spectral_product(left_side, right_side):
    return jnp.stack(
        [
            left_side[0] * right_side[0] - left_side[1] * right_side[1],
            left_side[0] * right_side[1] + left_side[1] * right_side[0],
        ]
    )


def adjoint_product(left_side, right_side):
    return jnp.stack(
        [
            left_side[0] * right_side[0] + left_side[1] * right_side[1],
            left_side[0] * right_side[1] - left_side[1] * right_side[0],
        ]
    )


def local_forward(stacked):
    local_freqs, frames, channels = (stacked.shape[1], stacked.shape[2], stacked.shape[3])
    inner_len = math.gcd(frames, 128)
    outer_len = frames // inner_len
    data = stacked.reshape(2, local_freqs, outer_len, inner_len, channels)
    cosine_table, sine_table = angle_table(outer_len, outer_len, outer_len)
    data = outer_pair(cosine_table, sine_table, data, "ga", "kabw", "kgbw", -1.0)
    cosine_table, sine_table = angle_table(outer_len, inner_len, frames)
    data = rotate_stacked(data, cosine_table[None, :, :, None], sine_table[None, :, :, None], -1.0)
    cosine_table, sine_table = angle_table(inner_len, inner_len, inner_len)
    data = dft_pair(cosine_table, sine_table, data, "fb", "kgbw", "kgfw", -1.0)
    return data.reshape(2, local_freqs, frames, channels)


def local_inverse(stacked):
    local_freqs, frames, channels = (stacked.shape[1], stacked.shape[2], stacked.shape[3])
    inner_len = math.gcd(frames, 128)
    outer_len = frames // inner_len
    data = stacked.reshape(2, local_freqs, outer_len, inner_len, channels)
    cosine_table, sine_table = angle_table(inner_len, inner_len, inner_len)
    data = dft_pair(cosine_table, sine_table, data, "bf", "kgfw", "kgbw", 1.0)
    cosine_table, sine_table = angle_table(outer_len, inner_len, frames)
    data = rotate_stacked(data, cosine_table[None, :, :, None], sine_table[None, :, :, None], 1.0)
    cosine_table, sine_table = angle_table(outer_len, outer_len, outer_len)
    data = outer_pair(cosine_table, sine_table, data, "ag", "kgbw", "kabw", 1.0)
    return data.reshape(2, local_freqs, frames, channels) / frames


def forward_gather(field):
    seq_devices = lax.axis_size("seq")
    frames, channels = field.shape
    block_rows = frames // seq_devices
    return lax.all_to_all(
        field.reshape(seq_devices, block_rows, channels),
        "seq",
        split_axis=0,
        concat_axis=0,
        tiled=True,
    )


def forward_transform(field):
    return forward_core(forward_gather(field))


def forward_core(received):
    seq_devices = lax.axis_size("seq")
    block_rows = received.shape[1]
    frames = seq_devices * block_rows
    freq_rows = 2 * seq_devices
    fft_length = freq_rows * frames
    values = received.astype(jnp.float32)
    cosine_table, sine_table = angle_table(seq_devices, seq_devices, freq_rows)
    alternating = jnp.where(jnp.arange(seq_devices) % 2 == 0, 1.0, -1.0).astype(jnp.float32)
    part_table = jnp.stack([cosine_table, (-sine_table).at[0].set(alternating)])
    section = jnp.einsum("ykq,qrw->ykrw", part_table, values, precision=PRECISE)
    frame_ids = lax.axis_index("seq") * block_rows + jnp.arange(block_rows, dtype=jnp.int32)
    products = (
        jnp.arange(seq_devices, dtype=jnp.int32)[:, None] * frame_ids[None, :] % fft_length
    )
    angles = products.astype(jnp.float32) * (FULL_TURN / fft_length)
    stacked = rotate_stacked(
        section, jnp.cos(angles)[:, :, None], jnp.sin(angles)[:, :, None], -1.0
    ).astype(jnp.bfloat16)
    regrouped = lax.all_to_all(stacked, "seq", split_axis=1, concat_axis=2, tiled=True)
    data = regrouped[:, 0].astype(jnp.float32)
    first_device = lax.axis_index("seq") == 0
    products = seq_devices * jnp.arange(frames, dtype=jnp.int32) % fft_length
    angles = (products.astype(jnp.float32) * (FULL_TURN / fft_length))[:, None]
    zeros = jnp.zeros_like(data[0])
    row_low = jnp.where(first_device, jnp.stack([data[0], zeros]), data)
    row_high = jnp.where(
        first_device,
        jnp.stack([jnp.cos(angles) * data[1], -jnp.sin(angles) * data[1]]),
        jnp.zeros_like(data),
    )
    return local_forward(jnp.stack([row_low, row_high], axis=1))


def inverse_core(spectra):
    seq_devices = lax.axis_size("seq")
    local_freqs, frames, channels = (spectra.shape[1], spectra.shape[2], spectra.shape[3])
    block_rows = frames // seq_devices
    freq_rows = 2 * seq_devices
    fft_length = freq_rows * frames
    stacked = local_inverse(spectra)
    device = lax.axis_index("seq")
    freq_ids = jnp.stack([device, jnp.int32(seq_devices)]).astype(jnp.int32)
    products = freq_ids[:, None] * jnp.arange(frames, dtype=jnp.int32)[None, :] % fft_length
    angles = products.astype(jnp.float32) * (FULL_TURN / fft_length)
    stacked = rotate_stacked(stacked, jnp.cos(angles)[:, :, None], jnp.sin(angles)[:, :, None], 1.0)
    back = stacked.astype(jnp.bfloat16)
    packed = jnp.where(device == 0, jnp.stack([back[0, 0], back[0, 1]]), back[:, 0])
    regrouped = lax.all_to_all(
        packed[:, None], "seq", split_axis=2, concat_axis=1, tiled=True
    ).astype(jnp.float32)
    cosine_table, sine_table = angle_table(seq_devices, seq_devices, freq_rows)
    alternating = jnp.where(jnp.arange(seq_devices) % 2 == 0, 1.0, -1.0).astype(jnp.float32)
    real_table = (2.0 * cosine_table).at[:, 0].set(1.0)
    imag_table = (-2.0 * sine_table).at[:, 0].set(alternating)
    part_table = jnp.stack([real_table, imag_table]) / freq_rows
    return jnp.einsum("zqk,zkrw->qrw", part_table, regrouped, precision=PRECISE)


def inverse_scatter(values):
    seq_devices, block_rows, channels = values.shape
    returned = lax.all_to_all(
        values.astype(jnp.bfloat16), "seq", split_axis=0, concat_axis=1, tiled=True
    )
    return returned.reshape(seq_devices * block_rows, channels)


def inverse_transform(spectra, keep_wide):
    return inverse_scatter(inverse_core(spectra))


def shards(frames_in, proj_weight, conv_taps, long_filters, out_grad):
    signal = frames_in[0]
    frames, channels = signal.shape
    seq_devices = lax.axis_size("seq")
    data_devices = lax.axis_size("dp")
    grad_scale = 1.0 / math.sqrt(data_devices * seq_devices * frames)
    margin_rows = conv_taps.shape[0] - 1
    tap_count = conv_taps.shape[0]
    projected = jnp.dot(signal, proj_weight, preferred_element_type=jnp.float32).astype(
        jnp.bfloat16
    )
    before = passed_along(projected[frames - margin_rows :], "seq", 1)
    extended = jnp.concatenate([before, projected], axis=0).astype(jnp.float32)
    mixed = sum(
        (
            conv_taps[tap_index][None, :]
            * extended[margin_rows - tap_index : margin_rows - tap_index + frames]
            for tap_index in range(tap_count)
        )
    ).astype(jnp.bfloat16)
    value = mixed[:, :channels]
    gate_one = mixed[:, channels : 2 * channels].astype(jnp.float32)
    gate_two = mixed[:, 2 * channels :].astype(jnp.float32)
    upstream = out_grad[0].astype(jnp.float32)
    grad_two = (upstream * gate_two).astype(jnp.bfloat16)
    opening_rows = forward_gather(
        jnp.concatenate(
            [
                long_filters.reshape(frames, 2 * channels),
                value,
                grad_two,
                mixed[:, channels : 2 * channels],
            ],
            axis=1,
        )
    )
    opening = forward_core(opening_rows[..., : 4 * channels])
    gate_one_blocks = opening_rows[..., 4 * channels :].astype(jnp.float32)
    filter_one = opening[..., :channels]
    filter_two = opening[..., channels : 2 * channels]
    value_spectra = opening[..., 2 * channels : 3 * channels]
    two_spectra = opening[..., 3 * channels :]
    middle_rows = inverse_core(
        jnp.concatenate(
            [
                spectral_product(filter_one, value_spectra),
                adjoint_product(filter_two, two_spectra),
            ],
            axis=3,
        )
    ).astype(jnp.bfloat16)
    conv_one_blocks = middle_rows[..., :channels].astype(jnp.float32)
    grad_first_blocks = middle_rows[..., channels:].astype(jnp.float32)
    first = (gate_one_blocks * conv_one_blocks).astype(jnp.bfloat16)
    grad_one = (grad_first_blocks * gate_one_blocks).astype(jnp.bfloat16)
    middle = inverse_scatter((grad_first_blocks * conv_one_blocks).astype(jnp.bfloat16))
    second = forward_core(jnp.concatenate([first, grad_one], axis=2))
    first_spectra = second[..., :channels]
    one_spectra = second[..., channels:]
    closing = inverse_transform(
        jnp.concatenate(
            [
                spectral_product(filter_two, first_spectra),
                adjoint_product(filter_one, one_spectra),
                adjoint_product(value_spectra, one_spectra),
                adjoint_product(first_spectra, two_spectra),
            ],
            axis=3,
        ),
        False,
    )
    conv_two = closing[:, :channels]
    grad_value = closing[:, channels : 2 * channels]
    tap_rows = closing[:, 2 * channels :]
    block = channels // data_devices
    tap_blocks = tap_rows.reshape(frames, 2, data_devices, block).transpose(2, 1, 0, 3)
    tap_parts = lax.all_to_all(tap_blocks, "dp", split_axis=0, concat_axis=0, tiled=True)
    grad_filters = (
        jnp.sum(tap_parts.astype(jnp.float32), axis=0).transpose(1, 0, 2) * grad_scale
    )
    layer_out = (gate_two * conv_two.astype(jnp.float32)).astype(jnp.bfloat16)
    grad_mixed = jnp.concatenate(
        [
            grad_value.astype(jnp.float32),
            middle.astype(jnp.float32),
            upstream * conv_two.astype(jnp.float32),
        ],
        axis=1,
    ).astype(jnp.bfloat16)
    after_rows = passed_along(grad_mixed[:margin_rows], "seq", -1)
    grad_mixed_f = grad_mixed.astype(jnp.float32)
    grad_pad = jnp.concatenate([grad_mixed, after_rows], axis=0).astype(jnp.float32)
    grad_rows = sum(
        (
            conv_taps[tap_index][None, :] * grad_pad[tap_index : tap_index + frames]
            for tap_index in range(tap_count)
        )
    ).astype(jnp.bfloat16)
    taps_terms = jnp.stack(
        [
            jnp.sum(
                extended[margin_rows - tap_index : margin_rows - tap_index + frames] * grad_mixed_f,
                axis=0,
            )
            for tap_index in range(tap_count)
        ]
    )
    all_devices = data_devices * seq_devices
    taps_flat = taps_terms.reshape(all_devices, -1)
    lane = 128
    proj_terms = jnp.einsum("tc,tj->cj", signal, grad_rows, preferred_element_type=jnp.float32)
    row_block = proj_terms.shape[0] // all_devices
    proj_flat = proj_terms.reshape(all_devices, row_block * proj_terms.shape[1] // lane, lane)
    taps_row = jnp.pad(taps_flat, ((0, 0), (0, lane - taps_flat.shape[1])))[:, None, :]
    proj_parts = jnp.sum(
        lax.all_to_all(
            jnp.concatenate([proj_flat, taps_row], axis=1),
            ("dp", "seq"),
            split_axis=0,
            concat_axis=0,
            tiled=True,
        ),
        axis=0,
    )
    taps_share = proj_parts[-1, : taps_flat.shape[1]]
    taps_whole = lax.all_to_all(
        jnp.broadcast_to(taps_share[None], taps_flat.shape),
        ("dp", "seq"),
        split_axis=0,
        concat_axis=0,
        tiled=True,
    )
    grad_taps = taps_whole.reshape(taps_terms.shape) * grad_scale
    grad_proj = proj_parts[:-1].reshape(row_block, proj_terms.shape[1]) * grad_scale
    grad_in = jnp.einsum(
        "tj,dj->td", grad_rows, proj_weight, preferred_element_type=jnp.float32
    ).astype(jnp.bfloat16)
    return (layer_out[None], grad_in[None], grad_proj, grad_taps, grad_filters)


def solution(mesh):
    placed = (P("dp", "seq", None), P(), P(), P("seq", None, None), P("dp", "seq", None))
    return jax.shard_map(
        shards,
        mesh=mesh,
        in_specs=placed,
        out_specs=(
            P("dp", "seq", None),
            P("dp", "seq", None),
            P(("dp", "seq"), None),
            P(),
            P("seq", None, "dp"),
        ),
        check_vma=False,
    )
```

```python
import math

import jax
import jax.numpy as jnp
from jax import lax
from jax.sharding import PartitionSpec as P

PRECISE = lax.Precision.HIGH
FULL_TURN = 2.0 * math.pi


def passed_along(value, axis, by):
    size = lax.axis_size(axis)
    pairs = [(i, i + by) for i in range(size) if 0 <= i + by < size]
    return lax.ppermute(value, axis, pairs)


def angle_table(row_count, col_count, period):
    products = (
        jnp.arange(row_count, dtype=jnp.int32)[:, None]
        * jnp.arange(col_count, dtype=jnp.int32)[None, :]
        % period
    )
    angles = products.astype(jnp.float32) * (FULL_TURN / period)
    return (jnp.cos(angles), jnp.sin(angles))


def rotate_stacked(stacked, cosine_table, sine_table, direction):
    return jnp.stack(
        [
            stacked[0] * cosine_table - direction * stacked[1] * sine_table,
            stacked[1] * cosine_table + direction * stacked[0] * sine_table,
        ]
    )


def dft_pair(cosine_table, sine_table, stacked, table_part, data_part, result_side, direction):
    block_table = jnp.stack(
        [
            jnp.stack([cosine_table, -direction * sine_table]),
            jnp.stack([direction * sine_table, cosine_table]),
        ]
    )
    return jnp.einsum(
        "yz" + table_part + ",z" + data_part + "->y" + result_side,
        block_table,
        stacked,
        precision=PRECISE,
    )


def outer_pair(cosine_table, sine_table, stacked, table_part, data_part, result_side, direction):
    if stacked.shape[2] != 2:
        return dft_pair(
            cosine_table, sine_table, stacked, table_part, data_part, result_side, direction
        )
    return jnp.stack([stacked[:, :, 0] + stacked[:, :, 1], stacked[:, :, 0] - stacked[:, :, 1]], axis=2)


def spectral_product(left_side, right_side):
    return jnp.stack(
        [
            left_side[0] * right_side[0] - left_side[1] * right_side[1],
            left_side[0] * right_side[1] + left_side[1] * right_side[0],
        ]
    )


def adjoint_product(left_side, right_side):
    return jnp.stack(
        [
            left_side[0] * right_side[0] + left_side[1] * right_side[1],
            left_side[0] * right_side[1] - left_side[1] * right_side[0],
        ]
    )


def local_forward(stacked):
    local_freqs, frames, channels = (stacked.shape[1], stacked.shape[2], stacked.shape[3])
    inner_len = math.gcd(frames, 128)
    outer_len = frames // inner_len
    data = stacked.reshape(2, local_freqs, outer_len, inner_len, channels)
    cosine_table, sine_table = angle_table(outer_len, outer_len, outer_len)
    data = outer_pair(cosine_table, sine_table, data, "ga", "kabw", "kgbw", -1.0)
    cosine_table, sine_table = angle_table(outer_len, inner_len, frames)
    data = rotate_stacked(data, cosine_table[None, :, :, None], sine_table[None, :, :, None], -1.0)
    cosine_table, sine_table = angle_table(inner_len, inner_len, inner_len)
    data = dft_pair(cosine_table, sine_table, data, "fb", "kgbw", "kgfw", -1.0)
    return data.reshape(2, local_freqs, frames, channels)


def local_inverse(stacked):
    local_freqs, frames, channels = (stacked.shape[1], stacked.shape[2], stacked.shape[3])
    inner_len = math.gcd(frames, 128)
    outer_len = frames // inner_len
    data = stacked.reshape(2, local_freqs, outer_len, inner_len, channels)
    cosine_table, sine_table = angle_table(inner_len, inner_len, inner_len)
    data = dft_pair(cosine_table, sine_table, data, "bf", "kgfw", "kgbw", 1.0)
    cosine_table, sine_table = angle_table(outer_len, inner_len, frames)
    data = rotate_stacked(data, cosine_table[None, :, :, None], sine_table[None, :, :, None], 1.0)
    cosine_table, sine_table = angle_table(outer_len, outer_len, outer_len)
    data = outer_pair(cosine_table, sine_table, data, "ag", "kgbw", "kabw", 1.0)
    return data.reshape(2, local_freqs, frames, channels) / frames


def forward_gather(field):
    seq_devices = lax.axis_size("seq")
    frames, channels = field.shape
    block_rows = frames // seq_devices
    return lax.all_to_all(
        field.reshape(seq_devices, block_rows, channels),
        "seq",
        split_axis=0,
        concat_axis=0,
        tiled=True,
    )


def forward_transform(field):
    return forward_core(forward_gather(field))


def forward_core(received):
    seq_devices = lax.axis_size("seq")
    block_rows = received.shape[1]
    frames = seq_devices * block_rows
    freq_rows = 2 * seq_devices
    fft_length = freq_rows * frames
    values = received.astype(jnp.float32)
    cosine_table, sine_table = angle_table(seq_devices, seq_devices, freq_rows)
    alternating = jnp.where(jnp.arange(seq_devices) % 2 == 0, 1.0, -1.0).astype(jnp.float32)
    part_table = jnp.stack([cosine_table, (-sine_table).at[0].set(alternating)])
    section = jnp.einsum("ykq,qrw->ykrw", part_table, values, precision=PRECISE)
    frame_ids = lax.axis_index("seq") * block_rows + jnp.arange(block_rows, dtype=jnp.int32)
    products = (
        jnp.arange(seq_devices, dtype=jnp.int32)[:, None] * frame_ids[None, :] % fft_length
    )
    angles = products.astype(jnp.float32) * (FULL_TURN / fft_length)
    stacked = rotate_stacked(
        section, jnp.cos(angles)[:, :, None], jnp.sin(angles)[:, :, None], -1.0
    ).astype(jnp.bfloat16)
    regrouped = lax.all_to_all(stacked, "seq", split_axis=1, concat_axis=2, tiled=True)
    data = regrouped[:, 0].astype(jnp.float32)
    first_device = lax.axis_index("seq") == 0
    products = seq_devices * jnp.arange(frames, dtype=jnp.int32) % fft_length
    angles = (products.astype(jnp.float32) * (FULL_TURN / fft_length))[:, None]
    zeros = jnp.zeros_like(data[0])
    row_low = jnp.where(first_device, jnp.stack([data[0], zeros]), data)
    row_high = jnp.where(
        first_device,
        jnp.stack([jnp.cos(angles) * data[1], -jnp.sin(angles) * data[1]]),
        jnp.zeros_like(data),
    )
    return local_forward(jnp.stack([row_low, row_high], axis=1))


def inverse_core(spectra):
    seq_devices = lax.axis_size("seq")
    local_freqs, frames, channels = (spectra.shape[1], spectra.shape[2], spectra.shape[3])
    block_rows = frames // seq_devices
    freq_rows = 2 * seq_devices
    fft_length = freq_rows * frames
    stacked = local_inverse(spectra)
    device = lax.axis_index("seq")
    freq_ids = jnp.stack([device, jnp.int32(seq_devices)]).astype(jnp.int32)
    products = freq_ids[:, None] * jnp.arange(frames, dtype=jnp.int32)[None, :] % fft_length
    angles = products.astype(jnp.float32) * (FULL_TURN / fft_length)
    stacked = rotate_stacked(stacked, jnp.cos(angles)[:, :, None], jnp.sin(angles)[:, :, None], 1.0)
    back = stacked.astype(jnp.bfloat16)
    packed = jnp.where(device == 0, jnp.stack([back[0, 0], back[0, 1]]), back[:, 0])
    regrouped = lax.all_to_all(
        packed[:, None], "seq", split_axis=2, concat_axis=1, tiled=True
    ).astype(jnp.float32)
    cosine_table, sine_table = angle_table(seq_devices, seq_devices, freq_rows)
    alternating = jnp.where(jnp.arange(seq_devices) % 2 == 0, 1.0, -1.0).astype(jnp.float32)
    real_table = (2.0 * cosine_table).at[:, 0].set(1.0)
    imag_table = (-2.0 * sine_table).at[:, 0].set(alternating)
    part_table = jnp.stack([real_table, imag_table]) / freq_rows
    return jnp.einsum("zqk,zkrw->qrw", part_table, regrouped, precision=PRECISE)


def inverse_scatter(values):
    seq_devices, block_rows, channels = values.shape
    returned = lax.all_to_all(
        values.astype(jnp.bfloat16), "seq", split_axis=0, concat_axis=1, tiled=True
    )
    return returned.reshape(seq_devices * block_rows, channels)


def inverse_transform(spectra, keep_wide):
    return inverse_scatter(inverse_core(spectra))


def shards(frames_in, proj_weight, conv_taps, long_filters, out_grad):
    signal = frames_in[0]
    frames, channels = signal.shape
    seq_devices = lax.axis_size("seq")
    data_devices = lax.axis_size("dp")
    grad_scale = 1.0 / math.sqrt(data_devices * seq_devices * frames)
    margin_rows = conv_taps.shape[0] - 1
    tap_count = conv_taps.shape[0]
    projected = jnp.dot(signal, proj_weight, preferred_element_type=jnp.float32).astype(
        jnp.bfloat16
    )
    before = passed_along(projected[frames - margin_rows :], "seq", 1)
    extended = jnp.concatenate([before, projected], axis=0).astype(jnp.float32)
    mixed = sum(
        (
            conv_taps[tap_index][None, :]
            * extended[margin_rows - tap_index : margin_rows - tap_index + frames]
            for tap_index in range(tap_count)
        )
    ).astype(jnp.bfloat16)
    value = mixed[:, :channels]
    gate_one = mixed[:, channels : 2 * channels].astype(jnp.float32)
    gate_two = mixed[:, 2 * channels :].astype(jnp.float32)
    upstream = out_grad[0].astype(jnp.float32)
    grad_two = (upstream * gate_two).astype(jnp.bfloat16)
    filter_rows = forward_gather(long_filters.reshape(frames, 2 * channels))
    opening_rows = jnp.concatenate(
        [
            filter_rows,
            forward_gather(
                jnp.concatenate([value, grad_two, mixed[:, channels : 2 * channels]], axis=1)
            ),
        ],
        axis=2,
    )
    opening = forward_core(opening_rows[..., : 4 * channels])
    gate_one_blocks = opening_rows[..., 4 * channels :].astype(jnp.float32)
    filter_one = opening[..., :channels]
    filter_two = opening[..., channels : 2 * channels]
    value_spectra = opening[..., 2 * channels : 3 * channels]
    two_spectra = opening[..., 3 * channels :]
    middle_rows = inverse_core(
        jnp.concatenate(
            [
                spectral_product(filter_one, value_spectra),
                adjoint_product(filter_two, two_spectra),
            ],
            axis=3,
        )
    ).astype(jnp.bfloat16)
    conv_one_blocks = middle_rows[..., :channels].astype(jnp.float32)
    grad_first_blocks = middle_rows[..., channels:].astype(jnp.float32)
    first = (gate_one_blocks * conv_one_blocks).astype(jnp.bfloat16)
    grad_one = (grad_first_blocks * gate_one_blocks).astype(jnp.bfloat16)
    middle = inverse_scatter((grad_first_blocks * conv_one_blocks).astype(jnp.bfloat16))
    second = forward_core(jnp.concatenate([first, grad_one], axis=2))
    first_spectra = second[..., :channels]
    one_spectra = second[..., channels:]
    closing = inverse_transform(
        jnp.concatenate(
            [
                spectral_product(filter_two, first_spectra),
                adjoint_product(filter_one, one_spectra),
                adjoint_product(value_spectra, one_spectra),
                adjoint_product(first_spectra, two_spectra),
            ],
            axis=3,
        ),
        False,
    )
    conv_two = closing[:, :channels]
    grad_value = closing[:, channels : 2 * channels]
    tap_rows = closing[:, 2 * channels :]
    block = channels // data_devices
    tap_blocks = tap_rows.reshape(frames, 2, data_devices, block).transpose(2, 1, 0, 3)
    tap_parts = lax.all_to_all(tap_blocks, "dp", split_axis=0, concat_axis=0, tiled=True)
    grad_filters = (
        jnp.sum(tap_parts.astype(jnp.float32), axis=0).transpose(1, 0, 2) * grad_scale
    )
    layer_out = (gate_two * conv_two.astype(jnp.float32)).astype(jnp.bfloat16)
    grad_mixed = jnp.concatenate(
        [
            grad_value.astype(jnp.float32),
            middle.astype(jnp.float32),
            upstream * conv_two.astype(jnp.float32),
        ],
        axis=1,
    ).astype(jnp.bfloat16)
    after_rows = passed_along(grad_mixed[:margin_rows], "seq", -1)
    grad_mixed_f = grad_mixed.astype(jnp.float32)
    grad_pad = jnp.concatenate([grad_mixed, after_rows], axis=0).astype(jnp.float32)
    grad_rows = sum(
        (
            conv_taps[tap_index][None, :] * grad_pad[tap_index : tap_index + frames]
            for tap_index in range(tap_count)
        )
    ).astype(jnp.bfloat16)
    taps_terms = jnp.stack(
        [
            jnp.sum(
                extended[margin_rows - tap_index : margin_rows - tap_index + frames] * grad_mixed_f,
                axis=0,
            )
            for tap_index in range(tap_count)
        ]
    )
    all_devices = data_devices * seq_devices
    taps_flat = taps_terms.reshape(all_devices, -1)
    lane = 128
    proj_terms = jnp.einsum("tc,tj->cj", signal, grad_rows, preferred_element_type=jnp.float32)
    row_block = proj_terms.shape[0] // all_devices
    proj_flat = proj_terms.reshape(all_devices, row_block * proj_terms.shape[1] // lane, lane)
    taps_row = jnp.pad(taps_flat, ((0, 0), (0, lane - taps_flat.shape[1])))[:, None, :]
    proj_parts = jnp.sum(
        lax.all_to_all(
            jnp.concatenate([proj_flat, taps_row], axis=1),
            ("dp", "seq"),
            split_axis=0,
            concat_axis=0,
            tiled=True,
        ),
        axis=0,
    )
    taps_share = proj_parts[-1, : taps_flat.shape[1]]
    taps_whole = lax.all_to_all(
        jnp.broadcast_to(taps_share[None], taps_flat.shape),
        ("dp", "seq"),
        split_axis=0,
        concat_axis=0,
        tiled=True,
    )
    grad_taps = taps_whole.reshape(taps_terms.shape) * grad_scale
    grad_proj = proj_parts[:-1].reshape(row_block, proj_terms.shape[1]) * grad_scale
    grad_in = jnp.einsum(
        "tj,dj->td", grad_rows, proj_weight, preferred_element_type=jnp.float32
    ).astype(jnp.bfloat16)
    return (layer_out[None], grad_in[None], grad_proj, grad_taps, grad_filters)


def solution(mesh):
    placed = (P("dp", "seq", None), P(), P(), P("seq", None, None), P("dp", "seq", None))
    return jax.shard_map(
        shards,
        mesh=mesh,
        in_specs=placed,
        out_specs=(
            P("dp", "seq", None),
            P("dp", "seq", None),
            P(("dp", "seq"), None),
            P(),
            P("seq", None, "dp"),
        ),
        check_vma=False,
    )
```

```python
import math

import jax
import jax.numpy as jnp
from jax import lax
from jax.sharding import PartitionSpec as P

PRECISE = lax.Precision.HIGH
FULL_TURN = 2.0 * math.pi


def passed_along(value, axis, by):
    size = lax.axis_size(axis)
    pairs = [(i, i + by) for i in range(size) if 0 <= i + by < size]
    return lax.ppermute(value, axis, pairs)


def angle_table(row_count, col_count, period):
    products = (
        jnp.arange(row_count, dtype=jnp.int32)[:, None]
        * jnp.arange(col_count, dtype=jnp.int32)[None, :]
        % period
    )
    angles = products.astype(jnp.float32) * (FULL_TURN / period)
    return (jnp.cos(angles), jnp.sin(angles))


def rotate_stacked(stacked, cosine_table, sine_table, direction):
    return jnp.stack(
        [
            stacked[0] * cosine_table - direction * stacked[1] * sine_table,
            stacked[1] * cosine_table + direction * stacked[0] * sine_table,
        ]
    )


def dft_pair(cosine_table, sine_table, stacked, table_part, data_part, result_side, direction):
    block_table = jnp.stack(
        [
            jnp.stack([cosine_table, -direction * sine_table]),
            jnp.stack([direction * sine_table, cosine_table]),
        ]
    )
    return jnp.einsum(
        "yz" + table_part + ",z" + data_part + "->y" + result_side,
        block_table,
        stacked,
        precision=PRECISE,
    )


def outer_pair(cosine_table, sine_table, stacked, table_part, data_part, result_side, direction):
    if stacked.shape[2] != 2:
        return dft_pair(
            cosine_table, sine_table, stacked, table_part, data_part, result_side, direction
        )
    return jnp.stack([stacked[:, :, 0] + stacked[:, :, 1], stacked[:, :, 0] - stacked[:, :, 1]], axis=2)


def spectral_product(left_side, right_side):
    return jnp.stack(
        [
            left_side[0] * right_side[0] - left_side[1] * right_side[1],
            left_side[0] * right_side[1] + left_side[1] * right_side[0],
        ]
    )


def adjoint_product(left_side, right_side):
    return jnp.stack(
        [
            left_side[0] * right_side[0] + left_side[1] * right_side[1],
            left_side[0] * right_side[1] - left_side[1] * right_side[0],
        ]
    )


def local_forward(stacked):
    local_freqs, frames, channels = (stacked.shape[1], stacked.shape[2], stacked.shape[3])
    inner_len = math.gcd(frames, 128)
    outer_len = frames // inner_len
    data = stacked.reshape(2, local_freqs, outer_len, inner_len, channels)
    cosine_table, sine_table = angle_table(outer_len, outer_len, outer_len)
    data = outer_pair(cosine_table, sine_table, data, "ga", "kabw", "kgbw", -1.0)
    cosine_table, sine_table = angle_table(outer_len, inner_len, frames)
    data = rotate_stacked(data, cosine_table[None, :, :, None], sine_table[None, :, :, None], -1.0)
    cosine_table, sine_table = angle_table(inner_len, inner_len, inner_len)
    data = dft_pair(cosine_table, sine_table, data, "fb", "kgbw", "kgfw", -1.0)
    return data.reshape(2, local_freqs, frames, channels)


def local_inverse(stacked):
    local_freqs, frames, channels = (stacked.shape[1], stacked.shape[2], stacked.shape[3])
    inner_len = math.gcd(frames, 128)
    outer_len = frames // inner_len
    data = stacked.reshape(2, local_freqs, outer_len, inner_len, channels)
    cosine_table, sine_table = angle_table(inner_len, inner_len, inner_len)
    data = dft_pair(cosine_table, sine_table, data, "bf", "kgfw", "kgbw", 1.0)
    cosine_table, sine_table = angle_table(outer_len, inner_len, frames)
    data = rotate_stacked(data, cosine_table[None, :, :, None], sine_table[None, :, :, None], 1.0)
    cosine_table, sine_table = angle_table(outer_len, outer_len, outer_len)
    data = outer_pair(cosine_table, sine_table, data, "ag", "kgbw", "kabw", 1.0)
    return data.reshape(2, local_freqs, frames, channels) / frames


def forward_gather(field):
    seq_devices = lax.axis_size("seq")
    frames, channels = field.shape
    block_rows = frames // seq_devices
    return lax.all_to_all(
        field.reshape(seq_devices, block_rows, channels),
        "seq",
        split_axis=0,
        concat_axis=0,
        tiled=True,
    )


def forward_transform(field):
    return forward_core(forward_gather(field))


def forward_core(received):
    seq_devices = lax.axis_size("seq")
    block_rows = received.shape[1]
    frames = seq_devices * block_rows
    freq_rows = 2 * seq_devices
    fft_length = freq_rows * frames
    values = received.astype(jnp.float32)
    cosine_table, sine_table = angle_table(seq_devices, seq_devices, freq_rows)
    alternating = jnp.where(jnp.arange(seq_devices) % 2 == 0, 1.0, -1.0).astype(jnp.float32)
    part_table = jnp.stack([cosine_table, (-sine_table).at[0].set(alternating)])
    section = jnp.einsum("ykq,qrw->ykrw", part_table, values, precision=PRECISE)
    frame_ids = lax.axis_index("seq") * block_rows + jnp.arange(block_rows, dtype=jnp.int32)
    products = (
        jnp.arange(seq_devices, dtype=jnp.int32)[:, None] * frame_ids[None, :] % fft_length
    )
    angles = products.astype(jnp.float32) * (FULL_TURN / fft_length)
    stacked = rotate_stacked(
        section, jnp.cos(angles)[:, :, None], jnp.sin(angles)[:, :, None], -1.0
    ).astype(jnp.bfloat16)
    regrouped = lax.all_to_all(stacked, "seq", split_axis=1, concat_axis=2, tiled=True)
    data = regrouped[:, 0].astype(jnp.float32)
    first_device = lax.axis_index("seq") == 0
    products = seq_devices * jnp.arange(frames, dtype=jnp.int32) % fft_length
    angles = (products.astype(jnp.float32) * (FULL_TURN / fft_length))[:, None]
    zeros = jnp.zeros_like(data[0])
    row_low = jnp.where(first_device, jnp.stack([data[0], zeros]), data)
    row_high = jnp.where(
        first_device,
        jnp.stack([jnp.cos(angles) * data[1], -jnp.sin(angles) * data[1]]),
        jnp.zeros_like(data),
    )
    return local_forward(jnp.stack([row_low, row_high], axis=1))


def inverse_core(spectra):
    seq_devices = lax.axis_size("seq")
    local_freqs, frames, channels = (spectra.shape[1], spectra.shape[2], spectra.shape[3])
    block_rows = frames // seq_devices
    freq_rows = 2 * seq_devices
    fft_length = freq_rows * frames
    stacked = local_inverse(spectra)
    device = lax.axis_index("seq")
    freq_ids = jnp.stack([device, jnp.int32(seq_devices)]).astype(jnp.int32)
    products = freq_ids[:, None] * jnp.arange(frames, dtype=jnp.int32)[None, :] % fft_length
    angles = products.astype(jnp.float32) * (FULL_TURN / fft_length)
    stacked = rotate_stacked(stacked, jnp.cos(angles)[:, :, None], jnp.sin(angles)[:, :, None], 1.0)
    back = stacked.astype(jnp.bfloat16)
    packed = jnp.where(device == 0, jnp.stack([back[0, 0], back[0, 1]]), back[:, 0])
    regrouped = lax.all_to_all(
        packed[:, None], "seq", split_axis=2, concat_axis=1, tiled=True
    ).astype(jnp.float32)
    cosine_table, sine_table = angle_table(seq_devices, seq_devices, freq_rows)
    alternating = jnp.where(jnp.arange(seq_devices) % 2 == 0, 1.0, -1.0).astype(jnp.float32)
    real_table = (2.0 * cosine_table).at[:, 0].set(1.0)
    imag_table = (-2.0 * sine_table).at[:, 0].set(alternating)
    part_table = jnp.stack([real_table, imag_table]) / freq_rows
    return jnp.einsum("zqk,zkrw->qrw", part_table, regrouped, precision=PRECISE)


def inverse_scatter(values):
    seq_devices, block_rows, channels = values.shape
    returned = lax.all_to_all(
        values.astype(jnp.bfloat16), "seq", split_axis=0, concat_axis=1, tiled=True
    )
    return returned.reshape(seq_devices * block_rows, channels)


def inverse_transform(spectra, keep_wide):
    return inverse_scatter(inverse_core(spectra))


def shards(frames_in, proj_weight, conv_taps, long_filters, out_grad):
    signal = frames_in[0]
    frames, channels = signal.shape
    seq_devices = lax.axis_size("seq")
    data_devices = lax.axis_size("dp")
    grad_scale = 1.0 / math.sqrt(data_devices * seq_devices * frames)
    margin_rows = conv_taps.shape[0] - 1
    tap_count = conv_taps.shape[0]
    projected = jnp.dot(signal, proj_weight, preferred_element_type=jnp.float32).astype(
        jnp.bfloat16
    )
    before = passed_along(projected[frames - margin_rows :], "seq", 1)
    extended = jnp.concatenate([before, projected], axis=0).astype(jnp.float32)
    mixed = sum(
        (
            conv_taps[tap_index][None, :]
            * extended[margin_rows - tap_index : margin_rows - tap_index + frames]
            for tap_index in range(tap_count)
        )
    ).astype(jnp.bfloat16)
    value = mixed[:, :channels]
    gate_one = mixed[:, channels : 2 * channels].astype(jnp.float32)
    gate_two = mixed[:, 2 * channels :].astype(jnp.float32)
    upstream = out_grad[0].astype(jnp.float32)
    grad_two = (upstream * gate_two).astype(jnp.bfloat16)
    opening_rows = forward_gather(
        jnp.concatenate(
            [
                long_filters.reshape(frames, 2 * channels),
                value,
                grad_two,
                mixed[:, channels : 2 * channels],
            ],
            axis=1,
        )
    )
    opening = forward_core(opening_rows[..., : 4 * channels])
    gate_one_blocks = opening_rows[..., 4 * channels :].astype(jnp.float32)
    filter_one = opening[..., :channels]
    filter_two = opening[..., channels : 2 * channels]
    value_spectra = opening[..., 2 * channels : 3 * channels]
    two_spectra = opening[..., 3 * channels :]
    middle_rows = inverse_core(
        jnp.concatenate(
            [
                spectral_product(filter_one, value_spectra),
                adjoint_product(filter_two, two_spectra),
            ],
            axis=3,
        )
    ).astype(jnp.bfloat16)
    conv_one_blocks = middle_rows[..., :channels].astype(jnp.float32)
    grad_first_blocks = middle_rows[..., channels:].astype(jnp.float32)
    first = (gate_one_blocks * conv_one_blocks).astype(jnp.bfloat16)
    grad_one = (grad_first_blocks * gate_one_blocks).astype(jnp.bfloat16)
    middle = inverse_scatter((grad_first_blocks * conv_one_blocks).astype(jnp.bfloat16))
    second = forward_core(jnp.concatenate([first, grad_one], axis=2))
    first_spectra = second[..., :channels]
    one_spectra = second[..., channels:]
    closing_blocks = inverse_core(
        jnp.concatenate(
            [
                spectral_product(filter_two, first_spectra),
                adjoint_product(filter_one, one_spectra),
                adjoint_product(value_spectra, one_spectra),
                adjoint_product(first_spectra, two_spectra),
            ],
            axis=3,
        ),
    )
    closing = inverse_scatter(closing_blocks[..., : 2 * channels])
    conv_two = closing[:, :channels]
    grad_value = closing[:, channels : 2 * channels]
    tap_rows = inverse_scatter(closing_blocks[..., 2 * channels :])
    block = channels // data_devices
    tap_blocks = tap_rows.reshape(frames, 2, data_devices, block).transpose(2, 1, 0, 3)
    tap_parts = lax.all_to_all(tap_blocks, "dp", split_axis=0, concat_axis=0, tiled=True)
    grad_filters = (
        jnp.sum(tap_parts.astype(jnp.float32), axis=0).transpose(1, 0, 2) * grad_scale
    )
    layer_out = (gate_two * conv_two.astype(jnp.float32)).astype(jnp.bfloat16)
    grad_mixed = jnp.concatenate(
        [
            grad_value.astype(jnp.float32),
            middle.astype(jnp.float32),
            upstream * conv_two.astype(jnp.float32),
        ],
        axis=1,
    ).astype(jnp.bfloat16)
    after_rows = passed_along(grad_mixed[:margin_rows], "seq", -1)
    grad_mixed_f = grad_mixed.astype(jnp.float32)
    grad_pad = jnp.concatenate([grad_mixed, after_rows], axis=0).astype(jnp.float32)
    grad_rows = sum(
        (
            conv_taps[tap_index][None, :] * grad_pad[tap_index : tap_index + frames]
            for tap_index in range(tap_count)
        )
    ).astype(jnp.bfloat16)
    taps_terms = jnp.stack(
        [
            jnp.sum(
                extended[margin_rows - tap_index : margin_rows - tap_index + frames] * grad_mixed_f,
                axis=0,
            )
            for tap_index in range(tap_count)
        ]
    )
    all_devices = data_devices * seq_devices
    taps_flat = taps_terms.reshape(all_devices, -1)
    lane = 128
    proj_terms = jnp.einsum("tc,tj->cj", signal, grad_rows, preferred_element_type=jnp.float32)
    row_block = proj_terms.shape[0] // all_devices
    proj_flat = proj_terms.reshape(all_devices, row_block * proj_terms.shape[1] // lane, lane)
    taps_row = jnp.pad(taps_flat, ((0, 0), (0, lane - taps_flat.shape[1])))[:, None, :]
    proj_parts = jnp.sum(
        lax.all_to_all(
            jnp.concatenate([proj_flat, taps_row], axis=1),
            ("dp", "seq"),
            split_axis=0,
            concat_axis=0,
            tiled=True,
        ),
        axis=0,
    )
    taps_share = proj_parts[-1, : taps_flat.shape[1]]
    taps_whole = lax.all_to_all(
        jnp.broadcast_to(taps_share[None], taps_flat.shape),
        ("dp", "seq"),
        split_axis=0,
        concat_axis=0,
        tiled=True,
    )
    grad_taps = taps_whole.reshape(taps_terms.shape) * grad_scale
    grad_proj = proj_parts[:-1].reshape(row_block, proj_terms.shape[1]) * grad_scale
    grad_in = jnp.einsum(
        "tj,dj->td", grad_rows, proj_weight, preferred_element_type=jnp.float32
    ).astype(jnp.bfloat16)
    return (layer_out[None], grad_in[None], grad_proj, grad_taps, grad_filters)


def solution(mesh):
    placed = (P("dp", "seq", None), P(), P(), P("seq", None, None), P("dp", "seq", None))
    return jax.shard_map(
        shards,
        mesh=mesh,
        in_specs=placed,
        out_specs=(
            P("dp", "seq", None),
            P("dp", "seq", None),
            P(("dp", "seq"), None),
            P(),
            P("seq", None, "dp"),
        ),
        check_vma=False,
    )
```
